256 devices in a mesh: dp: 8 (over x, core), seq: 32 (over y, z).
Axes of the slice: x: 4, y: 4, z: 8, core: 2. Of those that a mesh axis runs over, the one named last changes fastest.
Arguments:
- voxels: bfloat16 [8, 4096, 4096], P('dp', 'seq'), may hold values from -6 to 6
- patch_weight: bfloat16 [4096, 1024], replicated, may hold values from -0.09375 to 0.09375
- patch_bias: float32 [1024], replicated, may hold values from -3 to 3
- enc_position: bfloat16 [4096, 1024], P('seq'), may hold values from -5 to 5
- visible: int32 [8, 4096], P('dp', 'seq'), may hold values from 0 to 1, as said below
- enc_project: bfloat16 [1024, 3072], P(('dp', 'seq')), may hold values from -1 to 1
- enc_merge: bfloat16 [1024, 1024], P(('dp', 'seq')), may hold values from -0.1875 to 0.1875
- dec_lift: bfloat16 [1024, 512], P(('dp', 'seq')), may hold values from -0.1875 to 0.1875
- mask_token: float32 [512], replicated, may hold values from -4 to 4
- dec_position: bfloat16 [4096, 512], P('seq'), may hold values from -5 to 5
- dec_project: bfloat16 [512, 1536], P(('dp', 'seq')), may hold values from -1 to 1
- dec_merge: bfloat16 [512, 512], P(('dp', 'seq')), may hold values from -0.25 to 0.25
- dec_predict: bfloat16 [512, 4096], P(('dp', 'seq')), may hold values from -0.25 to 0.25
Outputs:
- decoded: bfloat16 [8, 4096, 512], P('dp', 'seq')
- patch_loss: float32 [8, 4096], P('dp', 'seq')
The draws below stay inside these ranges and needn't reach their ends.
Inputs may be any that keep to these rules, and one draw needn't show every extreme that they name: `visible`: each cube has exactly 1024 ones. Each slab of 128 consecutive patches holds between 0 and 64 ones, and in every cube some slab holds exactly 64.
All inputs are finite; a program needn't handle non-finite values.
Results may differ from the reference program's by a relative error of at most 0.008.
Values may be sent and summed in bfloat16 or wider, within the bound.
No kernel may reach another device: no remote copies, remote signals or barrier semaphores. Data moves between devices by JAX's collectives and lax.ppermute only.
A program may use at most 128 MiB of HBM per device.

```python
import math
import jax
import jax.numpy as jnp
from jax import lax

D = 1024
ENC_HEADS = 16
DEC = 512
DEC_HEADS = 16
PATCH = 4096
TOK_DEV = 128
TOKENS = 4096
CUBES = 8
VIS = 1024


def draw_visible(key, part):
    slabs = TOKENS // TOK_DEV
    half_slabs = slabs // 2
    quarter = TOK_DEV // 4
    key_swing, key_order, key_pick = jax.random.split(jax.random.fold_in(key, 7), 3)
    swing = jax.random.randint(key_swing, (CUBES, half_slabs), 0, quarter + 1)
    swing = swing.at[:, 0].set(quarter)
    paired = jnp.concatenate([quarter + swing, quarter - swing], axis=1)
    orders = jax.vmap(lambda k: jax.random.permutation(k, slabs))(jax.random.split(key_order, CUBES))
    counts = jnp.take_along_axis(paired, orders, axis=1)
    ranks = jax.vmap(lambda k: jax.random.permutation(k, TOK_DEV))(jax.random.split(key_pick, CUBES * slabs))
    ranks = ranks.reshape(CUBES, slabs, TOK_DEV)
    chosen = (ranks < counts[:, :, None]).astype(jnp.int32)
    return chosen.reshape(CUBES, TOKENS)


def position_noise(key, salt, rows, width):
    noise = 0.5 * jax.random.normal(jax.random.fold_in(key, salt + 1), (rows, width), jnp.float32)
    return jnp.clip(noise, -3.0, 3.0)


def project_base(key, salt, width):
    noise = jax.random.normal(jax.random.fold_in(key, salt + 3), (width, 3 * width), jnp.float32)
    return jnp.clip(noise, -6.0, 6.0) / math.sqrt(width)


def draw_enc_position(key, part):
    values = position_noise(key, 101, TOKENS, D)
    return values.astype(jnp.bfloat16)


def draw_dec_position(key, part):
    values = position_noise(key, 201, TOKENS, DEC)
    return values.astype(jnp.bfloat16)


def draw_enc_project(key, part):
    values = project_base(key, 101, D)
    return values.astype(jnp.bfloat16)


def draw_dec_project(key, part):
    values = project_base(key, 201, DEC)
    return values.astype(jnp.bfloat16)


def block_levels(own_key, shape, cuts, low, top_value):
    def one(dim, parts):
        heights = jax.random.uniform(jax.random.fold_in(jax.random.fold_in(own_key, 6), dim), (parts,), jnp.float32, low / len(cuts), top_value / len(cuts))
        return jnp.repeat(jnp.exp(heights), shape[dim] // parts).reshape((-1,) + (1,) * (len(shape) - dim - 1))

    level = one(*cuts[0])
    for cut in cuts[1:]:
        level = level * one(*cut)
    return level


def centred(own_key, shape, scale, most, pieces=(), held_as=jnp.bfloat16):
    array = jax.random.normal(own_key, shape, jnp.float32) * scale
    if len(pieces) > 0:
        array = block_levels(own_key, shape, pieces, -0.22, 0.18) * array
    return jnp.clip(array, min=-most, max=most).astype(held_as)


def setup_inputs(seed: int = 0) -> dict:
    key_list = jax.random.split(jax.random.key(seed), 14)
    voxels = centred(key_list[0], (CUBES, TOKENS, PATCH), 1.0, 6.0, ((0, 8), (1, 32)))
    patch_weight = centred(key_list[1], (PATCH, D), PATCH ** -0.5, 0.09375)
    patch_bias = centred(key_list[2], (D,), 0.5, 3.0, (), jnp.float32)
    enc_position = draw_enc_position(jax.random.fold_in(key_list[13], 71), 0)
    visible = draw_visible(jax.random.fold_in(key_list[13], 71), 0)
    enc_project = draw_enc_project(jax.random.fold_in(key_list[13], 71), 0)
    enc_merge = centred(key_list[6], (D, D), D ** -0.5, 0.1875, ((0, 256),))
    dec_lift = centred(key_list[7], (D, DEC), D ** -0.5, 0.1875, ((0, 256),))
    mask_token = centred(key_list[8], (DEC,), 1.0, 4.0, (), jnp.float32)
    dec_position = draw_dec_position(jax.random.fold_in(key_list[13], 71), 0)
    dec_project = draw_dec_project(jax.random.fold_in(key_list[13], 71), 0)
    dec_merge = centred(key_list[11], (DEC, DEC), DEC ** -0.5, 0.25, ((0, 256),))
    dec_predict = centred(key_list[12], (DEC, PATCH), DEC ** -0.5, 0.25, ((0, 256),))
    return dict(voxels=voxels, patch_weight=patch_weight, patch_bias=patch_bias, enc_position=enc_position, visible=visible, enc_project=enc_project, enc_merge=enc_merge, dec_lift=dec_lift, mask_token=mask_token, dec_position=dec_position, dec_project=dec_project, dec_merge=dec_merge, dec_predict=dec_predict)


def layer_norm(values):
    centre = values - lax.optimization_barrier(jnp.mean(values, axis=-1, keepdims=True))
    spread = lax.optimization_barrier(jnp.mean(centre * centre, axis=-1, keepdims=True))
    return centre * lax.rsqrt(spread + 1e-06)

def attention(packed, heads):
    row_count = packed.shape[0]
    piece_width = packed.shape[1] // 3
    head_size = piece_width // heads
    score_scale = 1.0 / math.sqrt(head_size)
    heads_split = packed.astype(jnp.float32).reshape(row_count, 3, heads, head_size).transpose(1, 2, 0, 3)

    def one_head(triple):
        queries, key_rows, value_rows = triple
        scores = jnp.einsum('qd,kd->qk', queries, key_rows) * score_scale
        top_score = lax.optimization_barrier(jnp.max(scores, axis=-1, keepdims=True))
        exponent = jnp.exp(scores - top_score)
        weights = (exponent / lax.optimization_barrier(jnp.sum(exponent, axis=-1, keepdims=True))).astype(jnp.bfloat16)
        return jnp.einsum('qk,kd->qd', weights.astype(jnp.float32), value_rows).astype(jnp.bfloat16)
    result = lax.map(one_head, (heads_split[0], heads_split[1], heads_split[2]))
    return result.transpose(1, 0, 2).reshape(row_count, piece_width)

def reference(voxels, patch_weight, patch_bias, enc_position, visible, enc_project, enc_merge, dec_lift, mask_token, dec_position, dec_project, dec_merge, dec_predict):

    def one_cube(cube_pair):
        cube_voxels, cube_flags = cube_pair
        embedded = (jnp.dot(cube_voxels, patch_weight, preferred_element_type=jnp.float32) + patch_bias + enc_position.astype(jnp.float32)).astype(jnp.bfloat16)
        kept_order = jnp.argsort(1 - cube_flags, stable=True)[:VIS].astype(jnp.int32)
        kept_rows = embedded[kept_order]
        enc_in = layer_norm(kept_rows.astype(jnp.float32)).astype(jnp.bfloat16)
        packed = jnp.dot(enc_in, enc_project, preferred_element_type=jnp.float32).astype(jnp.bfloat16)
        enc_mix = attention(packed, ENC_HEADS)
        encoded = kept_rows.astype(jnp.float32) + jnp.dot(enc_mix, enc_merge, preferred_element_type=jnp.float32)
        lifted = jnp.dot(layer_norm(encoded).astype(jnp.bfloat16), dec_lift, preferred_element_type=jnp.float32)
        filled = jnp.broadcast_to(mask_token, (TOKENS, DEC)).astype(jnp.float32)
        dec_in = (filled.at[kept_order].set(lifted) + dec_position.astype(jnp.float32)).astype(jnp.bfloat16)
        dec_packed = jnp.dot(layer_norm(dec_in.astype(jnp.float32)).astype(jnp.bfloat16), dec_project, preferred_element_type=jnp.float32).astype(jnp.bfloat16)
        dec_mix = attention(dec_packed, DEC_HEADS)
        decoded = (dec_in.astype(jnp.float32) + jnp.dot(dec_mix, dec_merge, preferred_element_type=jnp.float32)).astype(jnp.bfloat16)
        predicted = jnp.dot(layer_norm(decoded.astype(jnp.float32)).astype(jnp.bfloat16), dec_predict, preferred_element_type=jnp.float32)
        target = layer_norm(cube_voxels.astype(jnp.float32))
        squared = lax.optimization_barrier(jnp.mean((predicted - target) * (predicted - target), axis=-1))
        losses = jnp.where(cube_flags == 1, jnp.zeros_like(squared), squared)
        return (decoded, losses)
    decoded, patch_loss = lax.map(one_cube, (voxels, visible))
    return (decoded, patch_loss)
```

```python
import math

import jax
import jax.numpy as jnp
from jax import lax
from jax.sharding import PartitionSpec as P

ENC_HEADS = 16
DEC_HEADS = 16


def layer_norm(values):
    centre = values - jnp.mean(values, axis=-1, keepdims=True)
    spread = jnp.mean(centre * centre, axis=-1, keepdims=True)
    return centre * lax.rsqrt(spread + 1e-06)


def attend_rows(queries, key_rows, value_rows, key_ok):
    query_rows, local_heads, head_size = queries.shape
    block_rows = math.gcd(query_rows, 512)
    score_scale = 1.0 / math.sqrt(head_size)
    query_blocks = queries[:, 0].reshape(query_rows // block_rows, block_rows, head_size)
    keys_one = key_rows[:, 0]
    values_one = value_rows[:, 0]

    def one_block(query_block):
        scores = (
            jnp.einsum("qd,kd->qk", query_block, keys_one, preferred_element_type=jnp.float32)
            * score_scale
        )
        if key_ok is not None:
            scores = jnp.where(key_ok[None, :], scores, -1e30)
        top_score = jnp.max(scores, axis=-1, keepdims=True)
        exponent = jnp.exp(scores - top_score)
        weights = (exponent / jnp.sum(exponent, axis=-1, keepdims=True)).astype(jnp.bfloat16)
        return jnp.einsum(
            "qk,kd->qd", weights, values_one, preferred_element_type=jnp.float32
        ).astype(jnp.bfloat16)

    head_outputs = [lax.map(one_block, query_blocks).reshape(query_rows, head_size)]
    return jnp.stack(head_outputs, axis=1)


def spread_heads(packed, heads, seq_count):
    row_count = packed.shape[0]
    head_size = packed.shape[1] // (3 * heads)
    query_parts = max(seq_count // heads, 1)
    local_heads = max(heads // seq_count, 1)
    layout = packed.reshape(row_count, 3, heads, head_size)
    layout = jnp.repeat(layout, query_parts, axis=2)
    layout = layout.reshape(row_count, 3, seq_count, local_heads, head_size).transpose(
        2, 0, 1, 3, 4
    )
    return layout.reshape(seq_count, row_count, 3 * local_heads * head_size)


def attend_heads(incoming, key_ok, heads, query_part, query_parts):
    sources, row_count, triple_width = incoming.shape
    local_heads = max(heads // sources, 1)
    head_size = triple_width // (3 * local_heads)
    all_rows = sources * row_count
    layout = incoming.reshape(all_rows, 3, local_heads, head_size)
    query_rows = all_rows // query_parts
    queries = lax.dynamic_slice_in_dim(layout[:, 0], query_part * query_rows, query_rows, 0)
    return attend_rows(queries, layout[:, 1], layout[:, 2], key_ok)


def place_rows(mixed_part, all_rows, query_part, sources):
    query_rows = mixed_part.shape[0]
    flat_part = mixed_part.reshape(query_rows, -1)
    buffer = jnp.zeros((all_rows, flat_part.shape[1]), jnp.bfloat16)
    buffer = lax.dynamic_update_slice(buffer, flat_part, (query_part * query_rows, 0))
    return buffer.reshape(sources, all_rows // sources, flat_part.shape[1])


def collect_heads(returned, heads, query_parts):
    sources, row_count, piece_width = returned.shape
    local_heads = max(heads // sources, 1)
    head_size = piece_width // local_heads
    arranged = returned.reshape(sources, row_count, local_heads, head_size).transpose(1, 0, 2, 3)
    arranged = arranged.reshape(row_count, heads, query_parts, head_size)
    summed = jnp.sum(arranged.astype(jnp.float32), axis=2).astype(jnp.bfloat16)
    return summed.reshape(row_count, heads * head_size)


def gather_weights(pieces):
    flat = jnp.concatenate([piece.reshape(-1) for piece in pieces])
    every = lax.all_gather(flat, ("dp", "seq"), axis=0, tiled=False)
    wholes = []
    start = 0
    for piece in pieces:
        size = piece.size
        part = every[:, start : start + size].reshape(-1, piece.shape[1])
        wholes.append(part)
        start += size
    return wholes


def shards(
    voxels,
    patch_weight,
    patch_bias,
    enc_position,
    visible,
    enc_project,
    enc_merge,
    dec_lift,
    mask_token,
    dec_position,
    dec_project,
    dec_merge,
    dec_predict,
):
    seq_count = lax.axis_size("seq")
    seq_place = lax.axis_index("seq")
    enc_parts = max(seq_count // ENC_HEADS, 1)
    dec_parts = max(seq_count // DEC_HEADS, 1)
    enc_part = seq_place % enc_parts
    dec_part = seq_place % dec_parts
    (full_project, full_merge, full_lift, *dec_weights) = gather_weights(
        (enc_project, enc_merge, dec_lift, dec_project, dec_merge, dec_predict)
    )
    tok_local = voxels.shape[1]
    slab_max = tok_local // 2
    slot_ids = jnp.arange(slab_max, dtype=jnp.int32)
    cube_index = 0
    cube_flags = visible[cube_index]
    embedded = (
        jnp.dot(voxels[cube_index], patch_weight, preferred_element_type=jnp.float32)
        + patch_bias
        + enc_position.astype(jnp.float32)
    ).astype(jnp.bfloat16)
    ranking = jnp.cumsum(cube_flags) - 1
    slot_index = jnp.where(cube_flags == 1, ranking, slab_max)
    chooser = (slot_index[None, :] == slot_ids[:, None]).astype(jnp.bfloat16)
    kept_rows = jnp.dot(chooser, embedded, preferred_element_type=jnp.float32).astype(jnp.bfloat16)
    present = slot_ids < jnp.sum(cube_flags)
    packed = jnp.dot(
        layer_norm(kept_rows.astype(jnp.float32)).astype(jnp.bfloat16),
        full_project,
        preferred_element_type=jnp.float32,
    ).astype(jnp.bfloat16)
    key_marks = jnp.broadcast_to(present.astype(jnp.bfloat16)[None, :], (seq_count, slab_max))
    outgoing = spread_heads(packed, ENC_HEADS, seq_count)
    incoming = lax.all_to_all(outgoing, "seq", split_axis=0, concat_axis=0, tiled=True)
    in_marks = lax.all_to_all(key_marks, "seq", split_axis=0, concat_axis=0, tiled=True)
    key_ok = in_marks.reshape(-1) > 0.5
    mixed_part = attend_heads(incoming, key_ok, ENC_HEADS, enc_part, enc_parts)
    returning = place_rows(mixed_part, incoming.shape[0] * incoming.shape[1], enc_part, seq_count)
    returned = lax.all_to_all(returning, "seq", split_axis=0, concat_axis=0, tiled=True)
    mixed_rows = collect_heads(returned, ENC_HEADS, enc_parts)
    encoded = kept_rows.astype(jnp.float32) + jnp.dot(
        mixed_rows, full_merge, preferred_element_type=jnp.float32
    )
    lifted_list = [
        jnp.dot(
            layer_norm(encoded).astype(jnp.bfloat16), full_lift, preferred_element_type=jnp.float32
        )
    ]
    rank_list = [ranking]
    cube_index = 0
    cube_flags = visible[cube_index]
    taken_rows = jnp.take(
        lifted_list[cube_index], jnp.clip(rank_list[cube_index], 0, slab_max - 1), axis=0
    )
    dec_in = (
        jnp.where(cube_flags[:, None] == 1, taken_rows, mask_token[None, :])
        + dec_position.astype(jnp.float32)
    ).astype(jnp.bfloat16)
    dec_packed = jnp.dot(
        layer_norm(dec_in.astype(jnp.float32)).astype(jnp.bfloat16),
        dec_weights[0],
        preferred_element_type=jnp.float32,
    ).astype(jnp.bfloat16)
    outgoing = spread_heads(dec_packed, DEC_HEADS, seq_count)
    incoming = lax.all_to_all(outgoing, "seq", split_axis=0, concat_axis=0, tiled=True)
    mixed_part = attend_heads(incoming, None, DEC_HEADS, dec_part, dec_parts)
    returning = place_rows(mixed_part, incoming.shape[0] * incoming.shape[1], dec_part, seq_count)
    returned = lax.all_to_all(returning, "seq", split_axis=0, concat_axis=0, tiled=True)
    mixed_rows = collect_heads(returned, DEC_HEADS, dec_parts)
    decoded = (
        dec_in.astype(jnp.float32)
        + jnp.dot(mixed_rows, dec_weights[1], preferred_element_type=jnp.float32)
    ).astype(jnp.bfloat16)
    predicted = jnp.dot(
        layer_norm(decoded.astype(jnp.float32)).astype(jnp.bfloat16),
        dec_weights[2],
        preferred_element_type=jnp.float32,
    )
    target = layer_norm(voxels[cube_index].astype(jnp.float32))
    squared = jnp.mean((predicted - target) * (predicted - target), axis=-1)
    loss_list = [jnp.where(cube_flags == 1, jnp.zeros_like(squared), squared)]
    decoded_list = [decoded]
    return (jnp.stack(decoded_list), jnp.stack(loss_list))


def solution(mesh):
    return jax.shard_map(
        shards,
        mesh=mesh,
        in_specs=(
            P("dp", "seq", None),
            P(),
            P(),
            P("seq", None),
            P("dp", "seq"),
            P(("dp", "seq"), None),
            P(("dp", "seq"), None),
            P(("dp", "seq"), None),
            P(),
            P("seq", None),
            P(("dp", "seq"), None),
            P(("dp", "seq"), None),
            P(("dp", "seq"), None),
        ),
        out_specs=(P("dp", "seq", None), P("dp", "seq")),
        check_vma=False,
    )
```

```python
import math

import jax
import jax.numpy as jnp
from jax import lax
from jax.sharding import PartitionSpec as P

ENC_HEADS = 16
DEC_HEADS = 16


def layer_norm(values):
    centre = values - jnp.mean(values, axis=-1, keepdims=True)
    spread = jnp.mean(centre * centre, axis=-1, keepdims=True)
    return centre * lax.rsqrt(spread + 1e-06)


def attend_rows(queries, key_rows, value_rows, key_ok):
    query_rows, local_heads, head_size = queries.shape
    block_rows = math.gcd(query_rows, 512)
    score_scale = 1.0 / math.sqrt(head_size)
    query_blocks = queries[:, 0].reshape(query_rows // block_rows, block_rows, head_size)
    keys_one = key_rows[:, 0]
    values_one = value_rows[:, 0]

    def one_block(query_block):
        scores = (
            jnp.einsum("qd,kd->qk", query_block, keys_one, preferred_element_type=jnp.float32)
            * score_scale
        )
        if key_ok is not None:
            scores = jnp.where(key_ok[None, :], scores, -1e30)
        top_score = jnp.max(scores, axis=-1, keepdims=True)
        exponent = jnp.exp(scores - top_score)
        weights = (exponent / jnp.sum(exponent, axis=-1, keepdims=True)).astype(jnp.bfloat16)
        return jnp.einsum(
            "qk,kd->qd", weights, values_one, preferred_element_type=jnp.float32
        ).astype(jnp.bfloat16)

    head_outputs = [lax.map(one_block, query_blocks).reshape(query_rows, head_size)]
    return jnp.stack(head_outputs, axis=1)


def spread_heads(packed, heads, seq_count):
    row_count = packed.shape[0]
    head_size = packed.shape[1] // (3 * heads)
    query_parts = max(seq_count // heads, 1)
    local_heads = max(heads // seq_count, 1)
    layout = packed.reshape(row_count, 3, heads, head_size)
    layout = jnp.repeat(layout, query_parts, axis=2)
    layout = layout.reshape(row_count, 3, seq_count, local_heads, head_size).transpose(
        2, 0, 1, 3, 4
    )
    return layout.reshape(seq_count, row_count, 3 * local_heads * head_size)


def attend_heads(incoming, key_ok, heads, query_part, query_parts):
    sources, row_count, triple_width = incoming.shape
    local_heads = max(heads // sources, 1)
    head_size = triple_width // (3 * local_heads)
    all_rows = sources * row_count
    layout = incoming.reshape(all_rows, 3, local_heads, head_size)
    query_rows = all_rows // query_parts
    queries = lax.dynamic_slice_in_dim(layout[:, 0], query_part * query_rows, query_rows, 0)
    return attend_rows(queries, layout[:, 1], layout[:, 2], key_ok)


def place_rows(mixed_part, all_rows, query_part, sources):
    query_rows = mixed_part.shape[0]
    flat_part = mixed_part.reshape(query_rows, -1)
    buffer = jnp.zeros((all_rows, flat_part.shape[1]), jnp.bfloat16)
    buffer = lax.dynamic_update_slice(buffer, flat_part, (query_part * query_rows, 0))
    return buffer.reshape(sources, all_rows // sources, flat_part.shape[1])


def collect_heads(returned, heads, query_parts):
    sources, row_count, piece_width = returned.shape
    local_heads = max(heads // sources, 1)
    head_size = piece_width // local_heads
    arranged = returned.reshape(sources, row_count, local_heads, head_size).transpose(1, 0, 2, 3)
    arranged = arranged.reshape(row_count, heads, query_parts, head_size)
    summed = jnp.sum(arranged.astype(jnp.float32), axis=2).astype(jnp.bfloat16)
    return summed.reshape(row_count, heads * head_size)


def gather_weights(pieces):
    flat = jnp.concatenate([piece.reshape(-1) for piece in pieces])
    every = lax.all_gather(flat, ("dp", "seq"), axis=0, tiled=True)
    lane = 128
    sources = every.shape[0] // flat.shape[0]
    tiles = every.reshape(sources, flat.shape[0] // lane, lane)
    wholes = []
    start = 0
    for piece in pieces:
        size = piece.size
        part = tiles[:, start // lane : (start + size) // lane, :]
        wholes.append(part.reshape(sources * piece.shape[0], piece.shape[1]))
        start += size
    return wholes


def weight_dot(rows, weight):
    return jnp.dot(rows, weight, preferred_element_type=jnp.float32)


def shards(
    voxels,
    patch_weight,
    patch_bias,
    enc_position,
    visible,
    enc_project,
    enc_merge,
    dec_lift,
    mask_token,
    dec_position,
    dec_project,
    dec_merge,
    dec_predict,
):
    seq_count = lax.axis_size("seq")
    seq_place = lax.axis_index("seq")
    enc_parts = max(seq_count // ENC_HEADS, 1)
    dec_parts = max(seq_count // DEC_HEADS, 1)
    enc_part = seq_place % enc_parts
    dec_part = seq_place % dec_parts
    (full_project, full_merge, full_lift, *dec_weights) = gather_weights(
        (enc_project, enc_merge, dec_lift, dec_project, dec_merge, dec_predict)
    )
    tok_local = voxels.shape[1]
    slab_max = tok_local // 2
    slot_ids = jnp.arange(slab_max, dtype=jnp.int32)
    cube_index = 0
    cube_flags = visible[cube_index]
    embedded = (
        jnp.dot(voxels[cube_index], patch_weight, preferred_element_type=jnp.float32)
        + patch_bias
        + enc_position.astype(jnp.float32)
    ).astype(jnp.bfloat16)
    ranking = jnp.cumsum(cube_flags) - 1
    slot_index = jnp.where(cube_flags == 1, ranking, slab_max)
    chooser = (slot_index[None, :] == slot_ids[:, None]).astype(jnp.bfloat16)
    kept_rows = jnp.dot(chooser, embedded, preferred_element_type=jnp.float32).astype(jnp.bfloat16)
    present = slot_ids < jnp.sum(cube_flags)
    packed = weight_dot(
        layer_norm(kept_rows.astype(jnp.float32)).astype(jnp.bfloat16), full_project
    ).astype(jnp.bfloat16)
    key_marks = jnp.broadcast_to(present.astype(jnp.bfloat16)[None, :], (seq_count, slab_max))
    outgoing = spread_heads(packed, ENC_HEADS, seq_count)
    incoming = lax.all_to_all(outgoing, "seq", split_axis=0, concat_axis=0, tiled=True)
    in_marks = lax.all_to_all(key_marks, "seq", split_axis=0, concat_axis=0, tiled=True)
    key_ok = in_marks.reshape(-1) > 0.5
    mixed_part = attend_heads(incoming, key_ok, ENC_HEADS, enc_part, enc_parts)
    returning = place_rows(mixed_part, incoming.shape[0] * incoming.shape[1], enc_part, seq_count)
    returned = lax.all_to_all(returning, "seq", split_axis=0, concat_axis=0, tiled=True)
    mixed_rows = collect_heads(returned, ENC_HEADS, enc_parts)
    encoded = kept_rows.astype(jnp.float32) + weight_dot(mixed_rows, full_merge)
    lifted_list = [
        weight_dot(layer_norm(encoded).astype(jnp.bfloat16), full_lift)
    ]
    rank_list = [ranking]
    cube_index = 0
    cube_flags = visible[cube_index]
    taken_rows = jnp.take(
        lifted_list[cube_index], jnp.clip(rank_list[cube_index], 0, slab_max - 1), axis=0
    )
    dec_in = (
        jnp.where(cube_flags[:, None] == 1, taken_rows, mask_token[None, :])
        + dec_position.astype(jnp.float32)
    ).astype(jnp.bfloat16)
    dec_packed = weight_dot(
        layer_norm(dec_in.astype(jnp.float32)).astype(jnp.bfloat16), dec_weights[0]
    ).astype(jnp.bfloat16)
    outgoing = spread_heads(dec_packed, DEC_HEADS, seq_count)
    incoming = lax.all_to_all(outgoing, "seq", split_axis=0, concat_axis=0, tiled=True)
    mixed_part = attend_heads(incoming, None, DEC_HEADS, dec_part, dec_parts)
    returning = place_rows(mixed_part, incoming.shape[0] * incoming.shape[1], dec_part, seq_count)
    returned = lax.all_to_all(returning, "seq", split_axis=0, concat_axis=0, tiled=True)
    mixed_rows = collect_heads(returned, DEC_HEADS, dec_parts)
    decoded = (
        dec_in.astype(jnp.float32)
        + weight_dot(mixed_rows, dec_weights[1])
    ).astype(jnp.bfloat16)
    predicted = weight_dot(layer_norm(decoded.astype(jnp.float32)).astype(jnp.bfloat16), dec_weights[2])
    target = layer_norm(voxels[cube_index].astype(jnp.float32))
    squared = jnp.mean((predicted - target) * (predicted - target), axis=-1)
    loss_list = [jnp.where(cube_flags == 1, jnp.zeros_like(squared), squared)]
    decoded_list = [decoded]
    return (jnp.stack(decoded_list), jnp.stack(loss_list))


def solution(mesh):
    return jax.shard_map(
        shards,
        mesh=mesh,
        in_specs=(
            P("dp", "seq", None),
            P(),
            P(),
            P("seq", None),
            P("dp", "seq"),
            P(("dp", "seq"), None),
            P(("dp", "seq"), None),
            P(("dp", "seq"), None),
            P(),
            P("seq", None),
            P(("dp", "seq"), None),
            P(("dp", "seq"), None),
            P(("dp", "seq"), None),
        ),
        out_specs=(P("dp", "seq", None), P("dp", "seq")),
        check_vma=False,
    )
```

```python
import math

import jax
import jax.numpy as jnp
from jax import lax
from jax.sharding import PartitionSpec as P

ENC_HEADS = 16
DEC_HEADS = 16


def layer_norm(values):
    centre = values - jnp.mean(values, axis=-1, keepdims=True)
    spread = jnp.mean(centre * centre, axis=-1, keepdims=True)
    return centre * lax.rsqrt(spread + 1e-06)


def attend_rows(queries, key_rows, value_rows, key_ok):
    query_rows, local_heads, head_size = queries.shape
    block_rows = math.gcd(query_rows, 512)
    score_scale = 1.0 / math.sqrt(head_size)
    query_blocks = queries[:, 0].reshape(query_rows // block_rows, block_rows, head_size)
    keys_one = key_rows[:, 0]
    values_one = value_rows[:, 0]

    def one_block(query_block):
        scores = (
            jnp.einsum("qd,kd->qk", query_block, keys_one, preferred_element_type=jnp.float32)
            * score_scale
        )
        if key_ok is not None:
            scores = jnp.where(key_ok[None, :], scores, -1e30)
        top_score = jnp.max(scores, axis=-1, keepdims=True)
        exponent = jnp.exp(scores - top_score)
        weights = (exponent / jnp.sum(exponent, axis=-1, keepdims=True)).astype(jnp.bfloat16)
        return jnp.einsum(
            "qk,kd->qd", weights, values_one, preferred_element_type=jnp.float32
        ).astype(jnp.bfloat16)

    head_outputs = [lax.map(one_block, query_blocks).reshape(query_rows, head_size)]
    return jnp.stack(head_outputs, axis=1)


def spread_heads(packed, heads, seq_count):
    row_count = packed.shape[0]
    head_size = packed.shape[1] // (3 * heads)
    query_parts = max(seq_count // heads, 1)
    local_heads = max(heads // seq_count, 1)
    layout = packed.reshape(row_count, 3, heads, head_size)
    layout = jnp.repeat(layout, query_parts, axis=2)
    layout = layout.reshape(row_count, 3, seq_count, local_heads, head_size).transpose(
        2, 0, 1, 3, 4
    )
    return layout.reshape(seq_count, row_count, 3 * local_heads * head_size)


def attend_heads(incoming, key_ok, heads, query_part, query_parts):
    sources, row_count, triple_width = incoming.shape
    local_heads = max(heads // sources, 1)
    head_size = triple_width // (3 * local_heads)
    all_rows = sources * row_count
    layout = incoming.reshape(all_rows, 3, local_heads, head_size)
    query_rows = all_rows // query_parts
    queries = lax.dynamic_slice_in_dim(layout[:, 0], query_part * query_rows, query_rows, 0)
    return attend_rows(queries, layout[:, 1], layout[:, 2], key_ok)


def place_rows(mixed_part, all_rows, query_part, sources):
    query_rows = mixed_part.shape[0]
    flat_part = mixed_part.reshape(query_rows, -1)
    buffer = jnp.zeros((all_rows, flat_part.shape[1]), jnp.bfloat16)
    buffer = lax.dynamic_update_slice(buffer, flat_part, (query_part * query_rows, 0))
    return buffer.reshape(sources, all_rows // sources, flat_part.shape[1])


def collect_heads(returned, heads, query_parts):
    sources, row_count, piece_width = returned.shape
    local_heads = max(heads // sources, 1)
    head_size = piece_width // local_heads
    arranged = returned.reshape(sources, row_count, local_heads, head_size).transpose(1, 0, 2, 3)
    arranged = arranged.reshape(row_count, heads, query_parts, head_size)
    summed = jnp.sum(arranged.astype(jnp.float32), axis=2).astype(jnp.bfloat16)
    return summed.reshape(row_count, heads * head_size)


def gather_weights(pieces):
    flat = jnp.concatenate([piece.reshape(-1) for piece in pieces])
    every = lax.all_gather(flat, ("dp", "seq"), axis=0, tiled=True)
    lane = 128
    sources = every.shape[0] // flat.shape[0]
    tiles = every.reshape(sources, flat.shape[0] // lane, lane)
    wholes = []
    start = 0
    for piece in pieces:
        size = piece.size
        part = tiles[:, start // lane : (start + size) // lane, :]
        wholes.append(part.reshape(sources * piece.shape[0], piece.shape[1]))
        start += size
    return wholes


def weight_dot(rows, weight):
    return jnp.dot(rows, weight, preferred_element_type=jnp.float32)


def shards(
    voxels,
    patch_weight,
    patch_bias,
    enc_position,
    visible,
    enc_project,
    enc_merge,
    dec_lift,
    mask_token,
    dec_position,
    dec_project,
    dec_merge,
    dec_predict,
):
    seq_count = lax.axis_size("seq")
    seq_place = lax.axis_index("seq")
    enc_parts = max(seq_count // ENC_HEADS, 1)
    dec_parts = max(seq_count // DEC_HEADS, 1)
    enc_part = seq_place % enc_parts
    dec_part = seq_place % dec_parts
    (full_project, full_merge, full_lift, *dec_weights) = gather_weights(
        (enc_project, enc_merge, dec_lift, dec_project, dec_merge, dec_predict)
    )
    tok_local = voxels.shape[1]
    slab_max = tok_local // 2
    slot_ids = jnp.arange(slab_max, dtype=jnp.int32)
    cube_index = 0
    cube_flags = visible[cube_index]
    embedded = (
        jnp.dot(voxels[cube_index], patch_weight, preferred_element_type=jnp.float32)
        + patch_bias
        + enc_position.astype(jnp.float32)
    ).astype(jnp.bfloat16)
    ranking = jnp.cumsum(cube_flags) - 1
    slot_index = jnp.where(cube_flags == 1, ranking, slab_max)
    chooser = (slot_index[None, :] == slot_ids[:, None]).astype(jnp.bfloat16)
    kept_rows = jnp.dot(chooser, embedded, preferred_element_type=jnp.float32).astype(jnp.bfloat16)
    present = slot_ids < jnp.sum(cube_flags)
    packed = weight_dot(
        layer_norm(kept_rows.astype(jnp.float32)).astype(jnp.bfloat16), full_project
    ).astype(jnp.bfloat16)
    key_marks = jnp.broadcast_to(present.astype(jnp.bfloat16)[None, :], (seq_count, slab_max))
    outgoing = spread_heads(packed, ENC_HEADS, seq_count)
    incoming = lax.all_to_all(outgoing, "seq", split_axis=0, concat_axis=0, tiled=True)
    incoming, full_merge, full_lift, dec_weights[0] = lax.optimization_barrier(
        (incoming, full_merge, full_lift, dec_weights[0])
    )
    in_marks = lax.all_to_all(key_marks, "seq", split_axis=0, concat_axis=0, tiled=True)
    key_ok = in_marks.reshape(-1) > 0.5
    mixed_part = attend_heads(incoming, key_ok, ENC_HEADS, enc_part, enc_parts)
    returning = place_rows(mixed_part, incoming.shape[0] * incoming.shape[1], enc_part, seq_count)
    returned = lax.all_to_all(returning, "seq", split_axis=0, concat_axis=0, tiled=True)
    mixed_rows = collect_heads(returned, ENC_HEADS, enc_parts)
    encoded = kept_rows.astype(jnp.float32) + weight_dot(mixed_rows, full_merge)
    lifted_list = [
        weight_dot(layer_norm(encoded).astype(jnp.bfloat16), full_lift)
    ]
    rank_list = [ranking]
    cube_index = 0
    cube_flags = visible[cube_index]
    taken_rows = jnp.take(
        lifted_list[cube_index], jnp.clip(rank_list[cube_index], 0, slab_max - 1), axis=0
    )
    dec_in = (
        jnp.where(cube_flags[:, None] == 1, taken_rows, mask_token[None, :])
        + dec_position.astype(jnp.float32)
    ).astype(jnp.bfloat16)
    dec_packed = weight_dot(
        layer_norm(dec_in.astype(jnp.float32)).astype(jnp.bfloat16), dec_weights[0]
    ).astype(jnp.bfloat16)
    outgoing = spread_heads(dec_packed, DEC_HEADS, seq_count)
    incoming = lax.all_to_all(outgoing, "seq", split_axis=0, concat_axis=0, tiled=True)
    incoming, dec_weights[1], dec_weights[2] = lax.optimization_barrier(
        (incoming, dec_weights[1], dec_weights[2])
    )
    mixed_part = attend_heads(incoming, None, DEC_HEADS, dec_part, dec_parts)
    returning = place_rows(mixed_part, incoming.shape[0] * incoming.shape[1], dec_part, seq_count)
    returned = lax.all_to_all(returning, "seq", split_axis=0, concat_axis=0, tiled=True)
    mixed_rows = collect_heads(returned, DEC_HEADS, dec_parts)
    decoded = (
        dec_in.astype(jnp.float32)
        + weight_dot(mixed_rows, dec_weights[1])
    ).astype(jnp.bfloat16)
    predicted = weight_dot(layer_norm(decoded.astype(jnp.float32)).astype(jnp.bfloat16), dec_weights[2])
    target = layer_norm(voxels[cube_index].astype(jnp.float32))
    squared = jnp.mean((predicted - target) * (predicted - target), axis=-1)
    loss_list = [jnp.where(cube_flags == 1, jnp.zeros_like(squared), squared)]
    decoded_list = [decoded]
    return (jnp.stack(decoded_list), jnp.stack(loss_list))


def solution(mesh):
    return jax.shard_map(
        shards,
        mesh=mesh,
        in_specs=(
            P("dp", "seq", None),
            P(),
            P(),
            P("seq", None),
            P("dp", "seq"),
            P(("dp", "seq"), None),
            P(("dp", "seq"), None),
            P(("dp", "seq"), None),
            P(),
            P("seq", None),
            P(("dp", "seq"), None),
            P(("dp", "seq"), None),
            P(("dp", "seq"), None),
        ),
        out_specs=(P("dp", "seq", None), P("dp", "seq")),
        check_vma=False,
    )
```

```python
import math

import jax
import jax.numpy as jnp
from jax import lax
from jax.sharding import PartitionSpec as P

ENC_HEADS = 16
DEC_HEADS = 16


def layer_norm(values):
    centre = values - jnp.mean(values, axis=-1, keepdims=True)
    spread = jnp.mean(centre * centre, axis=-1, keepdims=True)
    return centre * lax.rsqrt(spread + 1e-06)


def attend_rows(queries, key_rows, value_rows, key_ok):
    query_rows, local_heads, head_size = queries.shape
    block_rows = math.gcd(query_rows, 512)
    score_scale = 1.0 / math.sqrt(head_size)
    query_blocks = queries[:, 0].reshape(query_rows // block_rows, block_rows, head_size)
    keys_one = key_rows[:, 0]
    values_one = value_rows[:, 0]

    def one_block(query_block):
        scores = (
            jnp.einsum("qd,kd->qk", query_block, keys_one, preferred_element_type=jnp.float32)
            * score_scale
        )
        if key_ok is not None:
            scores = jnp.where(key_ok[None, :], scores, -1e30)
        top_score = jnp.max(scores, axis=-1, keepdims=True)
        exponent = jnp.exp(scores - top_score)
        weights = (exponent / jnp.sum(exponent, axis=-1, keepdims=True)).astype(jnp.bfloat16)
        return jnp.einsum(
            "qk,kd->qd", weights, values_one, preferred_element_type=jnp.float32
        ).astype(jnp.bfloat16)

    head_outputs = [lax.map(one_block, query_blocks).reshape(query_rows, head_size)]
    return jnp.stack(head_outputs, axis=1)


def spread_heads(packed, heads, seq_count):
    row_count = packed.shape[0]
    head_size = packed.shape[1] // (3 * heads)
    query_parts = max(seq_count // heads, 1)
    local_heads = max(heads // seq_count, 1)
    layout = packed.reshape(row_count, 3, heads, head_size)
    layout = jnp.repeat(layout, query_parts, axis=2)
    layout = layout.reshape(row_count, 3, seq_count, local_heads, head_size).transpose(
        2, 0, 1, 3, 4
    )
    return layout.reshape(seq_count, row_count, 3 * local_heads * head_size)


def attend_heads(incoming, key_ok, heads, query_part, query_parts):
    sources, row_count, triple_width = incoming.shape
    local_heads = max(heads // sources, 1)
    head_size = triple_width // (3 * local_heads)
    all_rows = sources * row_count
    layout = incoming.reshape(all_rows, 3, local_heads, head_size)
    query_rows = all_rows // query_parts
    queries = lax.dynamic_slice_in_dim(layout[:, 0], query_part * query_rows, query_rows, 0)
    return attend_rows(queries, layout[:, 1], layout[:, 2], key_ok)


def place_rows(mixed_part, all_rows, query_part, sources):
    query_rows = mixed_part.shape[0]
    flat_part = mixed_part.reshape(query_rows, -1)
    buffer = jnp.zeros((all_rows, flat_part.shape[1]), jnp.bfloat16)
    buffer = lax.dynamic_update_slice(buffer, flat_part, (query_part * query_rows, 0))
    return buffer.reshape(sources, all_rows // sources, flat_part.shape[1])


def collect_heads(returned, heads, query_parts):
    sources, row_count, piece_width = returned.shape
    local_heads = max(heads // sources, 1)
    head_size = piece_width // local_heads
    arranged = returned.reshape(sources, row_count, local_heads, head_size).transpose(1, 0, 2, 3)
    arranged = arranged.reshape(row_count, heads, query_parts, head_size)
    summed = jnp.sum(arranged.astype(jnp.float32), axis=2).astype(jnp.bfloat16)
    return summed.reshape(row_count, heads * head_size)


def gather_weights(pieces):
    flat = jnp.concatenate([piece.reshape(-1) for piece in pieces])
    every = lax.all_gather(flat, ("dp", "seq"), axis=0, tiled=True)
    lane = 128
    sources = every.shape[0] // flat.shape[0]
    tiles = every.reshape(sources, flat.shape[0] // lane, lane)
    wholes = []
    start = 0
    for piece in pieces:
        size = piece.size
        part = tiles[:, start // lane : (start + size) // lane, :]
        wholes.append(part.reshape(sources * piece.shape[0], piece.shape[1]))
        start += size
    return wholes, tiles


def weight_dot(rows, weight):
    return jnp.dot(rows, weight, preferred_element_type=jnp.float32)


def head_columns(tiles, shape, heads, seq_count, seq_place):
    shard_rows, width = shape
    lane = tiles.shape[2]
    sources = tiles.shape[0]
    piece_width = width // 3
    head_size = piece_width // heads
    local_heads = max(heads // seq_count, 1)
    query_parts = max(seq_count // heads, 1)
    local = jnp.arange(local_heads, dtype=jnp.int32)
    head_ids = (seq_place * local_heads + local) // query_parts
    offsets = jnp.arange(head_size, dtype=jnp.int32)
    thirds = jnp.arange(3, dtype=jnp.int32)
    columns = (
        thirds[:, None, None] * piece_width
        + head_ids[None, :, None] * head_size
        + offsets[None, None, :]
    ).reshape(-1)
    shard_ids = jnp.arange(shard_rows, dtype=jnp.int32)
    groups = shard_ids[:, None] * (width // lane) + (columns // lane)[None, :]
    lanes = jnp.broadcast_to((columns % lane)[None, :], groups.shape)
    chosen = tiles[:, groups, lanes]
    return chosen.reshape(sources * shard_rows, columns.shape[0])


def shards(
    voxels,
    patch_weight,
    patch_bias,
    enc_position,
    visible,
    enc_project,
    enc_merge,
    dec_lift,
    mask_token,
    dec_position,
    dec_project,
    dec_merge,
    dec_predict,
):
    seq_count = lax.axis_size("seq")
    seq_place = lax.axis_index("seq")
    enc_parts = max(seq_count // ENC_HEADS, 1)
    dec_parts = max(seq_count // DEC_HEADS, 1)
    enc_part = seq_place % enc_parts
    dec_part = seq_place % dec_parts
    (_, full_merge, full_lift, *dec_weights), tiles = gather_weights(
        (enc_project, enc_merge, dec_lift, dec_project, dec_merge, dec_predict)
    )
    tok_local = voxels.shape[1]
    slab_max = tok_local // 2
    slot_ids = jnp.arange(slab_max, dtype=jnp.int32)
    cube_index = 0
    cube_flags = visible[cube_index]
    embedded = (
        jnp.dot(voxels[cube_index], patch_weight, preferred_element_type=jnp.float32)
        + patch_bias
        + enc_position.astype(jnp.float32)
    ).astype(jnp.bfloat16)
    ranking = jnp.cumsum(cube_flags) - 1
    slot_index = jnp.where(cube_flags == 1, ranking, slab_max)
    chooser = (slot_index[None, :] == slot_ids[:, None]).astype(jnp.bfloat16)
    kept_rows = jnp.dot(chooser, embedded, preferred_element_type=jnp.float32).astype(jnp.bfloat16)
    present = slot_ids < jnp.sum(cube_flags)
    enc_in = layer_norm(kept_rows.astype(jnp.float32)).astype(jnp.bfloat16)
    key_marks = jnp.broadcast_to(present.astype(jnp.bfloat16)[None, :], (seq_count, slab_max))
    spread_in = jnp.broadcast_to(enc_in[None], (seq_count,) + enc_in.shape)
    all_in = lax.all_to_all(spread_in, "seq", split_axis=0, concat_axis=0, tiled=True)
    head_project = head_columns(tiles, enc_project.shape, ENC_HEADS, seq_count, seq_place)
    incoming = jnp.dot(
        all_in.reshape(-1, all_in.shape[-1]), head_project, preferred_element_type=jnp.float32
    ).astype(jnp.bfloat16)
    incoming = incoming.reshape(seq_count, slab_max, head_project.shape[1])
    in_marks = lax.all_to_all(key_marks, "seq", split_axis=0, concat_axis=0, tiled=True)
    key_ok = in_marks.reshape(-1) > 0.5
    mixed_part = attend_heads(incoming, key_ok, ENC_HEADS, enc_part, enc_parts)
    returning = place_rows(mixed_part, incoming.shape[0] * incoming.shape[1], enc_part, seq_count)
    returned = lax.all_to_all(returning, "seq", split_axis=0, concat_axis=0, tiled=True)
    returned, full_merge, full_lift, dec_weights[0] = lax.optimization_barrier(
        (returned, full_merge, full_lift, dec_weights[0])
    )
    mixed_rows = collect_heads(returned, ENC_HEADS, enc_parts)
    encoded = kept_rows.astype(jnp.float32) + weight_dot(mixed_rows, full_merge)
    lifted_list = [
        weight_dot(layer_norm(encoded).astype(jnp.bfloat16), full_lift)
    ]
    rank_list = [ranking]
    cube_index = 0
    cube_flags = visible[cube_index]
    taken_rows = jnp.take(
        lifted_list[cube_index], jnp.clip(rank_list[cube_index], 0, slab_max - 1), axis=0
    )
    dec_in = (
        jnp.where(cube_flags[:, None] == 1, taken_rows, mask_token[None, :])
        + dec_position.astype(jnp.float32)
    ).astype(jnp.bfloat16)
    dec_packed = weight_dot(
        layer_norm(dec_in.astype(jnp.float32)).astype(jnp.bfloat16), dec_weights[0]
    ).astype(jnp.bfloat16)
    outgoing = spread_heads(dec_packed, DEC_HEADS, seq_count)
    incoming = lax.all_to_all(outgoing, "seq", split_axis=0, concat_axis=0, tiled=True)
    incoming, dec_weights[1], dec_weights[2] = lax.optimization_barrier(
        (incoming, dec_weights[1], dec_weights[2])
    )
    mixed_part = attend_heads(incoming, None, DEC_HEADS, dec_part, dec_parts)
    returning = place_rows(mixed_part, incoming.shape[0] * incoming.shape[1], dec_part, seq_count)
    returned = lax.all_to_all(returning, "seq", split_axis=0, concat_axis=0, tiled=True)
    mixed_rows = collect_heads(returned, DEC_HEADS, dec_parts)
    decoded = (
        dec_in.astype(jnp.float32)
        + weight_dot(mixed_rows, dec_weights[1])
    ).astype(jnp.bfloat16)
    predicted = weight_dot(layer_norm(decoded.astype(jnp.float32)).astype(jnp.bfloat16), dec_weights[2])
    target = layer_norm(voxels[cube_index].astype(jnp.float32))
    squared = jnp.mean((predicted - target) * (predicted - target), axis=-1)
    loss_list = [jnp.where(cube_flags == 1, jnp.zeros_like(squared), squared)]
    decoded_list = [decoded]
    return (jnp.stack(decoded_list), jnp.stack(loss_list))


def solution(mesh):
    return jax.shard_map(
        shards,
        mesh=mesh,
        in_specs=(
            P("dp", "seq", None),
            P(),
            P(),
            P("seq", None),
            P("dp", "seq"),
            P(("dp", "seq"), None),
            P(("dp", "seq"), None),
            P(("dp", "seq"), None),
            P(),
            P("seq", None),
            P(("dp", "seq"), None),
            P(("dp", "seq"), None),
            P(("dp", "seq"), None),
        ),
        out_specs=(P("dp", "seq", None), P("dp", "seq")),
        check_vma=False,
    )
```

```python
import functools
import math

import jax
import jax.numpy as jnp
from jax import lax
from jax.experimental import pallas as pl
from jax.sharding import PartitionSpec as P

ENC_HEADS = 16
DEC_HEADS = 16


def layer_norm(values):
    centre = values - jnp.mean(values, axis=-1, keepdims=True)
    spread = jnp.mean(centre * centre, axis=-1, keepdims=True)
    return centre * lax.rsqrt(spread + 1e-06)


def attention_kernel(mark_ref, query_ref, key_ref, value_ref, out_ref, *, score_scale):
    scores = (
        lax.dot_general(
            query_ref[...],
            key_ref[...],
            (((1,), (1,)), ((), ())),
            preferred_element_type=jnp.float32,
        )
        * score_scale
    )
    scores = jnp.where(mark_ref[...] > 0.5, scores, -1e30)
    top_score = jnp.max(scores, axis=-1, keepdims=True)
    exponent = jnp.exp(scores - top_score)
    weights = (exponent / jnp.sum(exponent, axis=-1, keepdims=True)).astype(jnp.bfloat16)
    out_ref[...] = jnp.dot(weights, value_ref[...], preferred_element_type=jnp.float32).astype(
        jnp.bfloat16
    )


def attend_rows(queries, key_rows, value_rows, key_ok):
    query_rows, local_heads, head_size = queries.shape
    key_count = key_rows.shape[0]
    block_rows = math.gcd(query_rows, 256)
    score_scale = 1.0 / math.sqrt(head_size)
    if key_ok is None:
        marks = jnp.ones((1, key_count), jnp.float32)
    else:
        marks = key_ok.astype(jnp.float32).reshape(1, key_count)
    whole = pl.BlockSpec((key_count, head_size), lambda step: (0, 0))
    mixed = pl.pallas_call(
        functools.partial(attention_kernel, score_scale=score_scale),
        grid=(query_rows // block_rows,),
        in_specs=[
            pl.BlockSpec((1, key_count), lambda step: (0, 0)),
            pl.BlockSpec((block_rows, head_size), lambda step: (step, 0)),
            whole,
            whole,
        ],
        out_specs=pl.BlockSpec((block_rows, head_size), lambda step: (step, 0)),
        out_shape=jax.ShapeDtypeStruct((query_rows, head_size), jnp.bfloat16),
    )(marks, queries[:, 0], key_rows[:, 0], value_rows[:, 0])
    return mixed[:, None, :]


def spread_heads(packed, heads, seq_count):
    row_count = packed.shape[0]
    head_size = packed.shape[1] // (3 * heads)
    query_parts = max(seq_count // heads, 1)
    local_heads = max(heads // seq_count, 1)
    layout = packed.reshape(row_count, 3, heads, head_size)
    layout = jnp.repeat(layout, query_parts, axis=2)
    layout = layout.reshape(row_count, 3, seq_count, local_heads, head_size).transpose(
        2, 0, 1, 3, 4
    )
    return layout.reshape(seq_count, row_count, 3 * local_heads * head_size)


def attend_heads(incoming, key_ok, heads, query_part, query_parts):
    sources, row_count, triple_width = incoming.shape
    local_heads = max(heads // sources, 1)
    head_size = triple_width // (3 * local_heads)
    all_rows = sources * row_count
    layout = incoming.reshape(all_rows, 3, local_heads, head_size)
    query_rows = all_rows // query_parts
    queries = lax.dynamic_slice_in_dim(layout[:, 0], query_part * query_rows, query_rows, 0)
    return attend_rows(queries, layout[:, 1], layout[:, 2], key_ok)


def place_rows(mixed_part, all_rows, query_part, sources):
    query_rows = mixed_part.shape[0]
    flat_part = mixed_part.reshape(query_rows, -1)
    buffer = jnp.zeros((all_rows, flat_part.shape[1]), jnp.bfloat16)
    buffer = lax.dynamic_update_slice(buffer, flat_part, (query_part * query_rows, 0))
    return buffer.reshape(sources, all_rows // sources, flat_part.shape[1])


def collect_heads(returned, heads, query_parts):
    sources, row_count, piece_width = returned.shape
    local_heads = max(heads // sources, 1)
    head_size = piece_width // local_heads
    arranged = returned.reshape(sources, row_count, local_heads, head_size).transpose(1, 0, 2, 3)
    arranged = arranged.reshape(row_count, heads, query_parts, head_size)
    summed = jnp.sum(arranged.astype(jnp.float32), axis=2).astype(jnp.bfloat16)
    return summed.reshape(row_count, heads * head_size)


def gather_weights(pieces):
    flat = jnp.concatenate([piece.reshape(-1) for piece in pieces])
    every = lax.all_gather(flat, ("dp", "seq"), axis=0, tiled=True)
    lane = 128
    sources = every.shape[0] // flat.shape[0]
    tiles = every.reshape(sources, flat.shape[0] // lane, lane)
    wholes = []
    start = 0
    for piece in pieces:
        size = piece.size
        part = tiles[:, start // lane : (start + size) // lane, :]
        wholes.append(part.reshape(sources * piece.shape[0], piece.shape[1]))
        start += size
    return wholes


def weight_dot(rows, weight):
    return jnp.dot(rows, weight, preferred_element_type=jnp.float32)


def shards(
    voxels,
    patch_weight,
    patch_bias,
    enc_position,
    visible,
    enc_project,
    enc_merge,
    dec_lift,
    mask_token,
    dec_position,
    dec_project,
    dec_merge,
    dec_predict,
):
    seq_count = lax.axis_size("seq")
    seq_place = lax.axis_index("seq")
    enc_parts = max(seq_count // ENC_HEADS, 1)
    dec_parts = max(seq_count // DEC_HEADS, 1)
    enc_part = seq_place % enc_parts
    dec_part = seq_place % dec_parts
    (full_project, full_merge, full_lift, *dec_weights) = gather_weights(
        (enc_project, enc_merge, dec_lift, dec_project, dec_merge, dec_predict)
    )
    tok_local = voxels.shape[1]
    slab_max = tok_local // 2
    slot_ids = jnp.arange(slab_max, dtype=jnp.int32)
    cube_index = 0
    cube_flags = visible[cube_index]
    embedded = (
        jnp.dot(voxels[cube_index], patch_weight, preferred_element_type=jnp.float32)
        + patch_bias
        + enc_position.astype(jnp.float32)
    ).astype(jnp.bfloat16)
    ranking = jnp.cumsum(cube_flags) - 1
    slot_index = jnp.where(cube_flags == 1, ranking, slab_max)
    chooser = (slot_index[None, :] == slot_ids[:, None]).astype(jnp.bfloat16)
    kept_rows = jnp.dot(chooser, embedded, preferred_element_type=jnp.float32).astype(jnp.bfloat16)
    present = slot_ids < jnp.sum(cube_flags)
    packed = weight_dot(
        layer_norm(kept_rows.astype(jnp.float32)).astype(jnp.bfloat16), full_project
    ).astype(jnp.bfloat16)
    key_marks = jnp.broadcast_to(present.astype(jnp.bfloat16)[None, :], (seq_count, slab_max))
    outgoing = spread_heads(packed, ENC_HEADS, seq_count)
    incoming = lax.all_to_all(outgoing, "seq", split_axis=0, concat_axis=0, tiled=True)
    incoming, full_merge, full_lift, dec_weights[0] = lax.optimization_barrier(
        (incoming, full_merge, full_lift, dec_weights[0])
    )
    in_marks = lax.all_to_all(key_marks, "seq", split_axis=0, concat_axis=0, tiled=True)
    key_ok = in_marks.reshape(-1) > 0.5
    mixed_part = attend_heads(incoming, key_ok, ENC_HEADS, enc_part, enc_parts)
    returning = place_rows(mixed_part, incoming.shape[0] * incoming.shape[1], enc_part, seq_count)
    returned = lax.all_to_all(returning, "seq", split_axis=0, concat_axis=0, tiled=True)
    mixed_rows = collect_heads(returned, ENC_HEADS, enc_parts)
    encoded = kept_rows.astype(jnp.float32) + weight_dot(mixed_rows, full_merge)
    lifted_list = [
        weight_dot(layer_norm(encoded).astype(jnp.bfloat16), full_lift)
    ]
    rank_list = [ranking]
    cube_index = 0
    cube_flags = visible[cube_index]
    taken_rows = jnp.take(
        lifted_list[cube_index], jnp.clip(rank_list[cube_index], 0, slab_max - 1), axis=0
    )
    dec_in = (
        jnp.where(cube_flags[:, None] == 1, taken_rows, mask_token[None, :])
        + dec_position.astype(jnp.float32)
    ).astype(jnp.bfloat16)
    dec_packed = weight_dot(
        layer_norm(dec_in.astype(jnp.float32)).astype(jnp.bfloat16), dec_weights[0]
    ).astype(jnp.bfloat16)
    outgoing = spread_heads(dec_packed, DEC_HEADS, seq_count)
    incoming = lax.all_to_all(outgoing, "seq", split_axis=0, concat_axis=0, tiled=True)
    incoming, dec_weights[1], dec_weights[2] = lax.optimization_barrier(
        (incoming, dec_weights[1], dec_weights[2])
    )
    mixed_part = attend_heads(incoming, None, DEC_HEADS, dec_part, dec_parts)
    returning = place_rows(mixed_part, incoming.shape[0] * incoming.shape[1], dec_part, seq_count)
    returned = lax.all_to_all(returning, "seq", split_axis=0, concat_axis=0, tiled=True)
    mixed_rows = collect_heads(returned, DEC_HEADS, dec_parts)
    decoded = (
        dec_in.astype(jnp.float32)
        + weight_dot(mixed_rows, dec_weights[1])
    ).astype(jnp.bfloat16)
    predicted = weight_dot(layer_norm(decoded.astype(jnp.float32)).astype(jnp.bfloat16), dec_weights[2])
    target = layer_norm(voxels[cube_index].astype(jnp.float32))
    squared = jnp.mean((predicted - target) * (predicted - target), axis=-1)
    loss_list = [jnp.where(cube_flags == 1, jnp.zeros_like(squared), squared)]
    decoded_list = [decoded]
    return (jnp.stack(decoded_list), jnp.stack(loss_list))


def solution(mesh):
    return jax.shard_map(
        shards,
        mesh=mesh,
        in_specs=(
            P("dp", "seq", None),
            P(),
            P(),
            P("seq", None),
            P("dp", "seq"),
            P(("dp", "seq"), None),
            P(("dp", "seq"), None),
            P(("dp", "seq"), None),
            P(),
            P("seq", None),
            P(("dp", "seq"), None),
            P(("dp", "seq"), None),
            P(("dp", "seq"), None),
        ),
        out_specs=(P("dp", "seq", None), P("dp", "seq")),
        check_vma=False,
    )
```

```python
import math

import jax
import jax.numpy as jnp
from jax import lax
from jax.sharding import PartitionSpec as P

ENC_HEADS = 16
DEC_HEADS = 16


def layer_norm(values):
    centre = values - jnp.mean(values, axis=-1, keepdims=True)
    spread = jnp.mean(centre * centre, axis=-1, keepdims=True)
    return centre * lax.rsqrt(spread + 1e-06)


def attend_rows(queries, key_rows, value_rows, key_ok):
    query_rows, local_heads, head_size = queries.shape
    block_rows = math.gcd(query_rows, 512)
    score_scale = 1.0 / math.sqrt(head_size)
    query_blocks = queries[:, 0].reshape(query_rows // block_rows, block_rows, head_size)
    keys_one = key_rows[:, 0]
    values_one = value_rows[:, 0]

    def one_block(query_block):
        scores = (
            jnp.einsum("qd,kd->qk", query_block, keys_one, preferred_element_type=jnp.float32)
            * score_scale
        )
        if key_ok is not None:
            scores = jnp.where(key_ok[None, :], scores, -1e30)
        top_score = jnp.max(scores, axis=-1, keepdims=True)
        exponent = jnp.exp(scores - top_score)
        weights = (exponent / jnp.sum(exponent, axis=-1, keepdims=True)).astype(jnp.bfloat16)
        return jnp.einsum(
            "qk,kd->qd", weights, values_one, preferred_element_type=jnp.float32
        ).astype(jnp.bfloat16)

    head_outputs = [lax.map(one_block, query_blocks).reshape(query_rows, head_size)]
    return jnp.stack(head_outputs, axis=1)


def spread_heads(packed, heads, seq_count):
    row_count = packed.shape[0]
    head_size = packed.shape[1] // (3 * heads)
    query_parts = max(seq_count // heads, 1)
    local_heads = max(heads // seq_count, 1)
    layout = packed.reshape(row_count, 3, heads, head_size)
    layout = jnp.repeat(layout, query_parts, axis=2)
    layout = layout.reshape(row_count, 3, seq_count, local_heads, head_size).transpose(
        2, 0, 1, 3, 4
    )
    return layout.reshape(seq_count, row_count, 3 * local_heads * head_size)


def attend_heads(incoming, key_ok, heads, query_part, query_parts):
    sources, row_count, triple_width = incoming.shape
    local_heads = max(heads // sources, 1)
    head_size = triple_width // (3 * local_heads)
    all_rows = sources * row_count
    layout = incoming.reshape(all_rows, 3, local_heads, head_size)
    query_rows = all_rows // query_parts
    queries = lax.dynamic_slice_in_dim(layout[:, 0], query_part * query_rows, query_rows, 0)
    return attend_rows(queries, layout[:, 1], layout[:, 2], key_ok)


def place_rows(mixed_part, all_rows, query_part, sources):
    query_rows = mixed_part.shape[0]
    flat_part = mixed_part.reshape(query_rows, -1)
    buffer = jnp.zeros((all_rows, flat_part.shape[1]), jnp.bfloat16)
    buffer = lax.dynamic_update_slice(buffer, flat_part, (query_part * query_rows, 0))
    return buffer.reshape(sources, all_rows // sources, flat_part.shape[1])


def collect_heads(returned, heads, query_parts):
    sources, row_count, piece_width = returned.shape
    local_heads = max(heads // sources, 1)
    head_size = piece_width // local_heads
    arranged = returned.reshape(sources, row_count, local_heads, head_size).transpose(1, 0, 2, 3)
    arranged = arranged.reshape(row_count, heads, query_parts, head_size)
    summed = jnp.sum(arranged.astype(jnp.float32), axis=2).astype(jnp.bfloat16)
    return summed.reshape(row_count, heads * head_size)


def send_rows(packed, heads, seq_count):
    row_count = packed.shape[0]
    head_size = packed.shape[1] // (3 * heads)
    query_parts = seq_count // heads
    part_rows = row_count // query_parts
    layout = packed.reshape(row_count, 3, heads, head_size)
    queries = layout[:, 0].reshape(query_parts, part_rows, heads, head_size).transpose(2, 0, 1, 3)
    queries = queries.reshape(seq_count, part_rows * head_size)
    pairs = layout[:, 1:].transpose(2, 0, 1, 3)
    pairs = jnp.broadcast_to(pairs[:, None], (heads, query_parts) + pairs.shape[1:])
    pairs = pairs.reshape(seq_count, row_count * 2 * head_size)
    return jnp.concatenate([queries, pairs], axis=1)


def attend_sent(incoming, key_ok, row_count, head_size):
    sources = incoming.shape[0]
    query_width = incoming.shape[1] - row_count * 2 * head_size
    queries = incoming[:, :query_width].reshape(-1, 1, head_size)
    pairs = incoming[:, query_width:].reshape(sources * row_count, 2, 1, head_size)
    mixed = attend_rows(queries, pairs[:, 0], pairs[:, 1], key_ok)
    return mixed.reshape(sources, query_width)


def take_back(returned, heads, row_count):
    seq_count = returned.shape[0]
    query_parts = seq_count // heads
    part_rows = row_count // query_parts
    head_size = returned.shape[1] // part_rows
    arranged = returned.reshape(heads, query_parts, part_rows, head_size).transpose(1, 2, 0, 3)
    return arranged.reshape(row_count, heads * head_size)


def gather_weights(pieces):
    flat = jnp.concatenate([piece.reshape(-1) for piece in pieces])
    every = lax.all_gather(flat, ("dp", "seq"), axis=0, tiled=True)
    lane = 128
    sources = every.shape[0] // flat.shape[0]
    tiles = every.reshape(sources, flat.shape[0] // lane, lane)
    wholes = []
    start = 0
    for piece in pieces:
        size = piece.size
        part = tiles[:, start // lane : (start + size) // lane, :]
        wholes.append(part.reshape(sources * piece.shape[0], piece.shape[1]))
        start += size
    return wholes


def weight_dot(rows, weight):
    return jnp.dot(rows, weight, preferred_element_type=jnp.float32)


def shards(
    voxels,
    patch_weight,
    patch_bias,
    enc_position,
    visible,
    enc_project,
    enc_merge,
    dec_lift,
    mask_token,
    dec_position,
    dec_project,
    dec_merge,
    dec_predict,
):
    seq_count = lax.axis_size("seq")
    seq_place = lax.axis_index("seq")
    enc_parts = max(seq_count // ENC_HEADS, 1)
    dec_parts = max(seq_count // DEC_HEADS, 1)
    enc_part = seq_place % enc_parts
    dec_part = seq_place % dec_parts
    (full_project, full_merge, full_lift, *dec_weights) = gather_weights(
        (enc_project, enc_merge, dec_lift, dec_project, dec_merge, dec_predict)
    )
    tok_local = voxels.shape[1]
    slab_max = tok_local // 2
    slot_ids = jnp.arange(slab_max, dtype=jnp.int32)
    cube_index = 0
    cube_flags = visible[cube_index]
    embedded = (
        jnp.dot(voxels[cube_index], patch_weight, preferred_element_type=jnp.float32)
        + patch_bias
        + enc_position.astype(jnp.float32)
    ).astype(jnp.bfloat16)
    ranking = jnp.cumsum(cube_flags) - 1
    slot_index = jnp.where(cube_flags == 1, ranking, slab_max)
    chooser = (slot_index[None, :] == slot_ids[:, None]).astype(jnp.bfloat16)
    kept_rows = jnp.dot(chooser, embedded, preferred_element_type=jnp.float32).astype(jnp.bfloat16)
    present = slot_ids < jnp.sum(cube_flags)
    packed = weight_dot(
        layer_norm(kept_rows.astype(jnp.float32)).astype(jnp.bfloat16), full_project
    ).astype(jnp.bfloat16)
    key_marks = jnp.broadcast_to(present.astype(jnp.bfloat16)[None, :], (seq_count, slab_max))
    outgoing = send_rows(packed, ENC_HEADS, seq_count)
    incoming = lax.all_to_all(outgoing, "seq", split_axis=0, concat_axis=0, tiled=True)
    incoming, full_merge, full_lift, dec_weights[0] = lax.optimization_barrier(
        (incoming, full_merge, full_lift, dec_weights[0])
    )
    in_marks = lax.all_to_all(key_marks, "seq", split_axis=0, concat_axis=0, tiled=True)
    key_ok = in_marks.reshape(-1) > 0.5
    enc_head_size = packed.shape[1] // (3 * ENC_HEADS)
    returning = attend_sent(incoming, key_ok, slab_max, enc_head_size)
    returned = lax.all_to_all(returning, "seq", split_axis=0, concat_axis=0, tiled=True)
    mixed_rows = take_back(returned, ENC_HEADS, slab_max)
    encoded = kept_rows.astype(jnp.float32) + weight_dot(mixed_rows, full_merge)
    lifted_list = [
        weight_dot(layer_norm(encoded).astype(jnp.bfloat16), full_lift)
    ]
    rank_list = [ranking]
    cube_index = 0
    cube_flags = visible[cube_index]
    taken_rows = jnp.take(
        lifted_list[cube_index], jnp.clip(rank_list[cube_index], 0, slab_max - 1), axis=0
    )
    dec_in = (
        jnp.where(cube_flags[:, None] == 1, taken_rows, mask_token[None, :])
        + dec_position.astype(jnp.float32)
    ).astype(jnp.bfloat16)
    dec_packed = weight_dot(
        layer_norm(dec_in.astype(jnp.float32)).astype(jnp.bfloat16), dec_weights[0]
    ).astype(jnp.bfloat16)
    outgoing = send_rows(dec_packed, DEC_HEADS, seq_count)
    incoming = lax.all_to_all(outgoing, "seq", split_axis=0, concat_axis=0, tiled=True)
    incoming, dec_weights[1], dec_weights[2] = lax.optimization_barrier(
        (incoming, dec_weights[1], dec_weights[2])
    )
    dec_head_size = dec_packed.shape[1] // (3 * DEC_HEADS)
    returning = attend_sent(incoming, None, tok_local, dec_head_size)
    returned = lax.all_to_all(returning, "seq", split_axis=0, concat_axis=0, tiled=True)
    mixed_rows = take_back(returned, DEC_HEADS, tok_local)
    decoded = (
        dec_in.astype(jnp.float32)
        + weight_dot(mixed_rows, dec_weights[1])
    ).astype(jnp.bfloat16)
    predicted = weight_dot(layer_norm(decoded.astype(jnp.float32)).astype(jnp.bfloat16), dec_weights[2])
    target = layer_norm(voxels[cube_index].astype(jnp.float32))
    squared = jnp.mean((predicted - target) * (predicted - target), axis=-1)
    loss_list = [jnp.where(cube_flags == 1, jnp.zeros_like(squared), squared)]
    decoded_list = [decoded]
    return (jnp.stack(decoded_list), jnp.stack(loss_list))


def solution(mesh):
    return jax.shard_map(
        shards,
        mesh=mesh,
        in_specs=(
            P("dp", "seq", None),
            P(),
            P(),
            P("seq", None),
            P("dp", "seq"),
            P(("dp", "seq"), None),
            P(("dp", "seq"), None),
            P(("dp", "seq"), None),
            P(),
            P("seq", None),
            P(("dp", "seq"), None),
            P(("dp", "seq"), None),
            P(("dp", "seq"), None),
        ),
        out_specs=(P("dp", "seq", None), P("dp", "seq")),
        check_vma=False,
    )
```

```python
import math

import jax
import jax.numpy as jnp
from jax import lax
from jax.sharding import PartitionSpec as P

ENC_HEADS = 16
DEC_HEADS = 16


def layer_norm(values):
    centre = values - jnp.mean(values, axis=-1, keepdims=True)
    spread = jnp.mean(centre * centre, axis=-1, keepdims=True)
    return centre * lax.rsqrt(spread + 1e-06)


def attend_rows(queries, key_rows, value_rows, key_ok):
    query_rows, local_heads, head_size = queries.shape
    block_rows = math.gcd(query_rows, 512)
    score_scale = 1.0 / math.sqrt(head_size)
    query_blocks = queries[:, 0].reshape(query_rows // block_rows, block_rows, head_size)
    keys_one = key_rows[:, 0]
    values_one = value_rows[:, 0]

    def one_block(query_block):
        scores = (
            jnp.einsum("qd,kd->qk", query_block, keys_one, preferred_element_type=jnp.float32)
            * score_scale
        )
        if key_ok is not None:
            scores = jnp.where(key_ok[None, :], scores, -1e30)
        top_score = jnp.max(scores, axis=-1, keepdims=True)
        exponent = jnp.exp(scores - top_score)
        weights = (exponent / jnp.sum(exponent, axis=-1, keepdims=True)).astype(jnp.bfloat16)
        return jnp.einsum(
            "qk,kd->qd", weights, values_one, preferred_element_type=jnp.float32
        ).astype(jnp.bfloat16)

    head_outputs = [lax.map(one_block, query_blocks).reshape(query_rows, head_size)]
    return jnp.stack(head_outputs, axis=1)


def spread_heads(packed, heads, seq_count):
    row_count = packed.shape[0]
    head_size = packed.shape[1] // (3 * heads)
    query_parts = max(seq_count // heads, 1)
    local_heads = max(heads // seq_count, 1)
    layout = packed.reshape(row_count, 3, heads, head_size)
    layout = jnp.repeat(layout, query_parts, axis=2)
    layout = layout.reshape(row_count, 3, seq_count, local_heads, head_size).transpose(
        2, 1, 0, 3, 4
    )
    return layout.reshape(seq_count, 3, row_count, local_heads * head_size)


def attend_heads(incoming, key_ok, heads, query_part, query_parts):
    sources, _, row_count, piece_width = incoming.shape
    local_heads = max(heads // sources, 1)
    head_size = piece_width // local_heads
    all_rows = sources * row_count
    thirds = [
        incoming[:, third].reshape(all_rows, local_heads, head_size) for third in range(3)
    ]
    query_rows = all_rows // query_parts
    queries = lax.dynamic_slice_in_dim(thirds[0], query_part * query_rows, query_rows, 0)
    return attend_rows(queries, thirds[1], thirds[2], key_ok)


def place_rows(mixed_part, all_rows, query_part, sources):
    query_rows = mixed_part.shape[0]
    flat_part = mixed_part.reshape(query_rows, -1)
    buffer = jnp.zeros((all_rows, flat_part.shape[1]), jnp.bfloat16)
    buffer = lax.dynamic_update_slice(buffer, flat_part, (query_part * query_rows, 0))
    return buffer.reshape(sources, all_rows // sources, flat_part.shape[1])


def collect_heads(returned, heads, query_parts):
    sources, row_count, piece_width = returned.shape
    local_heads = max(heads // sources, 1)
    head_size = piece_width // local_heads
    arranged = returned.reshape(sources, row_count, local_heads, head_size).transpose(1, 0, 2, 3)
    arranged = arranged.reshape(row_count, heads, query_parts, head_size)
    summed = jnp.sum(arranged.astype(jnp.float32), axis=2).astype(jnp.bfloat16)
    return summed.reshape(row_count, heads * head_size)


def gather_weights(pieces):
    flat = jnp.concatenate([piece.reshape(-1) for piece in pieces])
    every = lax.all_gather(flat, ("dp", "seq"), axis=0, tiled=True)
    lane = 128
    sources = every.shape[0] // flat.shape[0]
    tiles = every.reshape(sources, flat.shape[0] // lane, lane)
    wholes = []
    start = 0
    for piece in pieces:
        size = piece.size
        part = tiles[:, start // lane : (start + size) // lane, :]
        wholes.append(part.reshape(sources * piece.shape[0], piece.shape[1]))
        start += size
    return wholes


def weight_dot(rows, weight):
    return jnp.dot(rows, weight, preferred_element_type=jnp.float32)


def shards(
    voxels,
    patch_weight,
    patch_bias,
    enc_position,
    visible,
    enc_project,
    enc_merge,
    dec_lift,
    mask_token,
    dec_position,
    dec_project,
    dec_merge,
    dec_predict,
):
    seq_count = lax.axis_size("seq")
    seq_place = lax.axis_index("seq")
    enc_parts = max(seq_count // ENC_HEADS, 1)
    dec_parts = max(seq_count // DEC_HEADS, 1)
    enc_part = seq_place % enc_parts
    dec_part = seq_place % dec_parts
    (full_project, full_merge, full_lift, *dec_weights) = gather_weights(
        (enc_project, enc_merge, dec_lift, dec_project, dec_merge, dec_predict)
    )
    tok_local = voxels.shape[1]
    slab_max = tok_local // 2
    slot_ids = jnp.arange(slab_max, dtype=jnp.int32)
    cube_index = 0
    cube_flags = visible[cube_index]
    embedded = (
        jnp.dot(voxels[cube_index], patch_weight, preferred_element_type=jnp.float32)
        + patch_bias
        + enc_position.astype(jnp.float32)
    ).astype(jnp.bfloat16)
    ranking = jnp.cumsum(cube_flags) - 1
    slot_index = jnp.where(cube_flags == 1, ranking, slab_max)
    chooser = (slot_index[None, :] == slot_ids[:, None]).astype(jnp.bfloat16)
    kept_rows = jnp.dot(chooser, embedded, preferred_element_type=jnp.float32).astype(jnp.bfloat16)
    present = slot_ids < jnp.sum(cube_flags)
    packed = weight_dot(
        layer_norm(kept_rows.astype(jnp.float32)).astype(jnp.bfloat16), full_project
    ).astype(jnp.bfloat16)
    key_marks = jnp.broadcast_to(present.astype(jnp.bfloat16)[None, :], (seq_count, slab_max))
    outgoing = spread_heads(packed, ENC_HEADS, seq_count)
    incoming = lax.all_to_all(outgoing, "seq", split_axis=0, concat_axis=0, tiled=True)
    incoming, full_merge, full_lift, dec_weights[0] = lax.optimization_barrier(
        (incoming, full_merge, full_lift, dec_weights[0])
    )
    in_marks = lax.all_to_all(key_marks, "seq", split_axis=0, concat_axis=0, tiled=True)
    key_ok = in_marks.reshape(-1) > 0.5
    mixed_part = attend_heads(incoming, key_ok, ENC_HEADS, enc_part, enc_parts)
    returning = place_rows(mixed_part, incoming.shape[0] * incoming.shape[2], enc_part, seq_count)
    returned = lax.all_to_all(returning, "seq", split_axis=0, concat_axis=0, tiled=True)
    mixed_rows = collect_heads(returned, ENC_HEADS, enc_parts)
    encoded = kept_rows.astype(jnp.float32) + weight_dot(mixed_rows, full_merge)
    lifted_list = [
        weight_dot(layer_norm(encoded).astype(jnp.bfloat16), full_lift)
    ]
    rank_list = [ranking]
    cube_index = 0
    cube_flags = visible[cube_index]
    taken_rows = jnp.take(
        lifted_list[cube_index], jnp.clip(rank_list[cube_index], 0, slab_max - 1), axis=0
    )
    dec_in = (
        jnp.where(cube_flags[:, None] == 1, taken_rows, mask_token[None, :])
        + dec_position.astype(jnp.float32)
    ).astype(jnp.bfloat16)
    dec_packed = weight_dot(
        layer_norm(dec_in.astype(jnp.float32)).astype(jnp.bfloat16), dec_weights[0]
    ).astype(jnp.bfloat16)
    outgoing = spread_heads(dec_packed, DEC_HEADS, seq_count)
    incoming = lax.all_to_all(outgoing, "seq", split_axis=0, concat_axis=0, tiled=True)
    incoming, dec_weights[1], dec_weights[2] = lax.optimization_barrier(
        (incoming, dec_weights[1], dec_weights[2])
    )
    mixed_part = attend_heads(incoming, None, DEC_HEADS, dec_part, dec_parts)
    returning = place_rows(mixed_part, incoming.shape[0] * incoming.shape[2], dec_part, seq_count)
    returned = lax.all_to_all(returning, "seq", split_axis=0, concat_axis=0, tiled=True)
    mixed_rows = collect_heads(returned, DEC_HEADS, dec_parts)
    decoded = (
        dec_in.astype(jnp.float32)
        + weight_dot(mixed_rows, dec_weights[1])
    ).astype(jnp.bfloat16)
    predicted = weight_dot(layer_norm(decoded.astype(jnp.float32)).astype(jnp.bfloat16), dec_weights[2])
    target = layer_norm(voxels[cube_index].astype(jnp.float32))
    squared = jnp.mean((predicted - target) * (predicted - target), axis=-1)
    loss_list = [jnp.where(cube_flags == 1, jnp.zeros_like(squared), squared)]
    decoded_list = [decoded]
    return (jnp.stack(decoded_list), jnp.stack(loss_list))


def solution(mesh):
    return jax.shard_map(
        shards,
        mesh=mesh,
        in_specs=(
            P("dp", "seq", None),
            P(),
            P(),
            P("seq", None),
            P("dp", "seq"),
            P(("dp", "seq"), None),
            P(("dp", "seq"), None),
            P(("dp", "seq"), None),
            P(),
            P("seq", None),
            P(("dp", "seq"), None),
            P(("dp", "seq"), None),
            P(("dp", "seq"), None),
        ),
        out_specs=(P("dp", "seq", None), P("dp", "seq")),
        check_vma=False,
    )
```

```python
import math

import jax
import jax.numpy as jnp
from jax import lax
from jax.sharding import PartitionSpec as P

ENC_HEADS = 16
DEC_HEADS = 16


def layer_norm(values):
    centre = values - jnp.mean(values, axis=-1, keepdims=True)
    spread = jnp.mean(centre * centre, axis=-1, keepdims=True)
    return centre * lax.rsqrt(spread + 1e-06)


def attend_rows(queries, key_rows, value_rows, key_ok):
    query_rows, local_heads, head_size = queries.shape
    block_rows = math.gcd(query_rows, 512)
    score_scale = 1.0 / math.sqrt(head_size)
    query_blocks = queries[:, 0].reshape(query_rows // block_rows, block_rows, head_size)
    keys_one = key_rows[:, 0]
    values_one = value_rows[:, 0]

    def one_block(query_block):
        scores = (
            jnp.einsum("qd,kd->qk", query_block, keys_one, preferred_element_type=jnp.float32)
            * score_scale
        )
        if key_ok is not None:
            scores = jnp.where(key_ok[None, :], scores, -1e30)
        top_score = jnp.max(scores, axis=-1, keepdims=True)
        exponent = jnp.exp(scores - top_score)
        weights = (exponent / jnp.sum(exponent, axis=-1, keepdims=True)).astype(jnp.bfloat16)
        return jnp.einsum(
            "qk,kd->qd", weights, values_one, preferred_element_type=jnp.float32
        ).astype(jnp.bfloat16)

    head_outputs = [lax.map(one_block, query_blocks).reshape(query_rows, head_size)]
    return jnp.stack(head_outputs, axis=1)


def spread_heads(packed, heads, seq_count):
    row_count = packed.shape[0]
    head_size = packed.shape[1] // (3 * heads)
    query_parts = max(seq_count // heads, 1)
    local_heads = max(heads // seq_count, 1)
    layout = packed.reshape(row_count, 3, heads, head_size)
    layout = jnp.repeat(layout, query_parts, axis=2)
    layout = layout.reshape(row_count, 3, seq_count, local_heads, head_size).transpose(
        2, 1, 0, 3, 4
    )
    return layout.reshape(seq_count, 3, row_count, local_heads * head_size)


def attend_heads(incoming, key_ok, heads, query_part, query_parts):
    sources, _, row_count, piece_width = incoming.shape
    local_heads = max(heads // sources, 1)
    head_size = piece_width // local_heads
    all_rows = sources * row_count
    thirds = [
        incoming[:, third].reshape(all_rows, local_heads, head_size) for third in range(3)
    ]
    query_rows = all_rows // query_parts
    queries = lax.dynamic_slice_in_dim(thirds[0], query_part * query_rows, query_rows, 0)
    return attend_rows(queries, thirds[1], thirds[2], key_ok)


def place_rows(mixed_part, all_rows, query_part, sources):
    query_rows = mixed_part.shape[0]
    flat_part = mixed_part.reshape(query_rows, -1)
    buffer = jnp.zeros((all_rows, flat_part.shape[1]), jnp.bfloat16)
    buffer = lax.dynamic_update_slice(buffer, flat_part, (query_part * query_rows, 0))
    return buffer.reshape(sources, all_rows // sources, flat_part.shape[1])


def collect_heads(returned, heads, query_parts):
    sources, row_count, piece_width = returned.shape
    local_heads = max(heads // sources, 1)
    head_size = piece_width // local_heads
    arranged = returned.reshape(sources, row_count, local_heads, head_size).transpose(1, 0, 2, 3)
    arranged = arranged.reshape(row_count, heads, query_parts, head_size)
    summed = jnp.sum(arranged.astype(jnp.float32), axis=2).astype(jnp.bfloat16)
    return summed.reshape(row_count, heads * head_size)


def gather_weights(pieces):
    flat = jnp.concatenate([piece.reshape(-1) for piece in pieces])
    every = lax.all_gather(flat, ("dp", "seq"), axis=0, tiled=True)
    lane = 128
    sources = every.shape[0] // flat.shape[0]
    tiles = every.reshape(sources, flat.shape[0] // lane, lane)
    wholes = []
    start = 0
    for piece in pieces:
        size = piece.size
        part = tiles[:, start // lane : (start + size) // lane, :]
        wholes.append(part.reshape(sources * piece.shape[0], piece.shape[1]))
        start += size
    return wholes


def weight_dot(rows, weight):
    return jnp.dot(rows, weight, preferred_element_type=jnp.float32)


def shards(
    voxels,
    patch_weight,
    patch_bias,
    enc_position,
    visible,
    enc_project,
    enc_merge,
    dec_lift,
    mask_token,
    dec_position,
    dec_project,
    dec_merge,
    dec_predict,
):
    seq_count = lax.axis_size("seq")
    seq_place = lax.axis_index("seq")
    enc_parts = max(seq_count // ENC_HEADS, 1)
    dec_parts = max(seq_count // DEC_HEADS, 1)
    enc_part = seq_place % enc_parts
    dec_part = seq_place % dec_parts
    (full_project, full_merge, full_lift, *dec_weights) = gather_weights(
        (enc_project, enc_merge, dec_lift, dec_project, dec_merge, dec_predict)
    )
    tok_local = voxels.shape[1]
    slab_max = tok_local // 2
    slot_ids = jnp.arange(slab_max, dtype=jnp.int32)
    cube_index = 0
    cube_flags = visible[cube_index]
    embedded = (
        jnp.dot(voxels[cube_index], patch_weight, preferred_element_type=jnp.float32)
        + patch_bias
        + enc_position.astype(jnp.float32)
    ).astype(jnp.bfloat16)
    ranking = jnp.cumsum(cube_flags) - 1
    slot_index = jnp.where(cube_flags == 1, ranking, slab_max)
    chooser = (slot_index[None, :] == slot_ids[:, None]).astype(jnp.bfloat16)
    kept_rows = jnp.dot(chooser, embedded, preferred_element_type=jnp.float32).astype(jnp.bfloat16)
    present = slot_ids < jnp.sum(cube_flags)
    packed = weight_dot(
        layer_norm(kept_rows.astype(jnp.float32)).astype(jnp.bfloat16), full_project
    ).astype(jnp.bfloat16)
    key_marks = jnp.broadcast_to(present.astype(jnp.bfloat16)[None, :], (seq_count, slab_max))
    outgoing = spread_heads(packed, ENC_HEADS, seq_count)
    incoming = lax.all_to_all(outgoing, "seq", split_axis=0, concat_axis=0, tiled=True)
    incoming, full_merge, full_lift = lax.optimization_barrier((incoming, full_merge, full_lift))
    in_marks = lax.all_to_all(key_marks, "seq", split_axis=0, concat_axis=0, tiled=True)
    key_ok = in_marks.reshape(-1) > 0.5
    mixed_part = attend_heads(incoming, key_ok, ENC_HEADS, enc_part, enc_parts)
    returning = place_rows(mixed_part, incoming.shape[0] * incoming.shape[2], enc_part, seq_count)
    returned = lax.all_to_all(returning, "seq", split_axis=0, concat_axis=0, tiled=True)
    returned, dec_weights[0] = lax.optimization_barrier((returned, dec_weights[0]))
    mixed_rows = collect_heads(returned, ENC_HEADS, enc_parts)
    encoded = kept_rows.astype(jnp.float32) + weight_dot(mixed_rows, full_merge)
    lifted_list = [
        weight_dot(layer_norm(encoded).astype(jnp.bfloat16), full_lift)
    ]
    rank_list = [ranking]
    cube_index = 0
    cube_flags = visible[cube_index]
    taken_rows = jnp.take(
        lifted_list[cube_index], jnp.clip(rank_list[cube_index], 0, slab_max - 1), axis=0
    )
    dec_in = (
        jnp.where(cube_flags[:, None] == 1, taken_rows, mask_token[None, :])
        + dec_position.astype(jnp.float32)
    ).astype(jnp.bfloat16)
    dec_packed = weight_dot(
        layer_norm(dec_in.astype(jnp.float32)).astype(jnp.bfloat16), dec_weights[0]
    ).astype(jnp.bfloat16)
    outgoing = spread_heads(dec_packed, DEC_HEADS, seq_count)
    incoming = lax.all_to_all(outgoing, "seq", split_axis=0, concat_axis=0, tiled=True)
    incoming, dec_weights[2] = lax.optimization_barrier((incoming, dec_weights[2]))
    mixed_part = attend_heads(incoming, None, DEC_HEADS, dec_part, dec_parts)
    returning = place_rows(mixed_part, incoming.shape[0] * incoming.shape[2], dec_part, seq_count)
    returned = lax.all_to_all(returning, "seq", split_axis=0, concat_axis=0, tiled=True)
    returned, dec_weights[1] = lax.optimization_barrier((returned, dec_weights[1]))
    mixed_rows = collect_heads(returned, DEC_HEADS, dec_parts)
    decoded = (
        dec_in.astype(jnp.float32)
        + weight_dot(mixed_rows, dec_weights[1])
    ).astype(jnp.bfloat16)
    predicted = weight_dot(layer_norm(decoded.astype(jnp.float32)).astype(jnp.bfloat16), dec_weights[2])
    target = layer_norm(voxels[cube_index].astype(jnp.float32))
    squared = jnp.mean((predicted - target) * (predicted - target), axis=-1)
    loss_list = [jnp.where(cube_flags == 1, jnp.zeros_like(squared), squared)]
    decoded_list = [decoded]
    return (jnp.stack(decoded_list), jnp.stack(loss_list))


def solution(mesh):
    return jax.shard_map(
        shards,
        mesh=mesh,
        in_specs=(
            P("dp", "seq", None),
            P(),
            P(),
            P("seq", None),
            P("dp", "seq"),
            P(("dp", "seq"), None),
            P(("dp", "seq"), None),
            P(("dp", "seq"), None),
            P(),
            P("seq", None),
            P(("dp", "seq"), None),
            P(("dp", "seq"), None),
            P(("dp", "seq"), None),
        ),
        out_specs=(P("dp", "seq", None), P("dp", "seq")),
        check_vma=False,
    )
```

```python
import math

import jax
import jax.numpy as jnp
from jax import lax
from jax.sharding import PartitionSpec as P

ENC_HEADS = 16
DEC_HEADS = 16


def layer_norm(values):
    centre = values - jnp.mean(values, axis=-1, keepdims=True)
    spread = jnp.mean(centre * centre, axis=-1, keepdims=True)
    return centre * lax.rsqrt(spread + 1e-06)


def attend_rows(queries, key_rows, value_rows, key_ok):
    query_rows, local_heads, head_size = queries.shape
    block_rows = math.gcd(query_rows, 512)
    score_scale = 1.0 / math.sqrt(head_size)
    query_blocks = queries[:, 0].reshape(query_rows // block_rows, block_rows, head_size)
    keys_one = key_rows[:, 0]
    values_one = value_rows[:, 0]

    def one_block(query_block):
        scores = (
            jnp.einsum("qd,kd->qk", query_block, keys_one, preferred_element_type=jnp.float32)
            * score_scale
        )
        if key_ok is not None:
            scores = jnp.where(key_ok[None, :], scores, -1e30)
        top_score = jnp.max(scores, axis=-1, keepdims=True)
        exponent = jnp.exp(scores - top_score)
        weights = (exponent / jnp.sum(exponent, axis=-1, keepdims=True)).astype(jnp.bfloat16)
        return jnp.einsum(
            "qk,kd->qd", weights, values_one, preferred_element_type=jnp.float32
        ).astype(jnp.bfloat16)

    head_outputs = [lax.map(one_block, query_blocks).reshape(query_rows, head_size)]
    return jnp.stack(head_outputs, axis=1)


def spread_heads(packed, heads, seq_count):
    row_count = packed.shape[0]
    head_size = packed.shape[1] // (3 * heads)
    query_parts = max(seq_count // heads, 1)
    local_heads = max(heads // seq_count, 1)
    layout = packed.reshape(row_count, 3, heads, head_size)
    layout = jnp.repeat(layout, query_parts, axis=2)
    layout = layout.reshape(row_count, 3, seq_count, local_heads, head_size).transpose(
        2, 1, 0, 3, 4
    )
    return layout.reshape(seq_count, 3, row_count, local_heads * head_size)


def attend_heads(incoming, key_ok, heads, query_part, query_parts):
    sources, _, row_count, piece_width = incoming.shape
    local_heads = max(heads // sources, 1)
    head_size = piece_width // local_heads
    all_rows = sources * row_count
    thirds = [
        incoming[:, third].reshape(all_rows, local_heads, head_size) for third in range(3)
    ]
    query_rows = all_rows // query_parts
    queries = lax.dynamic_slice_in_dim(thirds[0], query_part * query_rows, query_rows, 0)
    return attend_rows(queries, thirds[1], thirds[2], key_ok)


def place_rows(mixed_part, all_rows, query_part, sources):
    query_rows = mixed_part.shape[0]
    flat_part = mixed_part.reshape(query_rows, -1)
    buffer = jnp.zeros((all_rows, flat_part.shape[1]), jnp.bfloat16)
    buffer = lax.dynamic_update_slice(buffer, flat_part, (query_part * query_rows, 0))
    return buffer.reshape(sources, all_rows // sources, flat_part.shape[1])


def collect_heads(returned, heads, query_parts):
    sources, row_count, piece_width = returned.shape
    local_heads = max(heads // sources, 1)
    head_size = piece_width // local_heads
    arranged = returned.reshape(sources, row_count, local_heads, head_size).transpose(1, 0, 2, 3)
    arranged = arranged.reshape(row_count, heads, query_parts, head_size)
    summed = jnp.sum(arranged.astype(jnp.float32), axis=2).astype(jnp.bfloat16)
    return summed.reshape(row_count, heads * head_size)


def gather_weights(pieces):
    flat = jnp.concatenate([piece.reshape(-1) for piece in pieces])
    every = lax.all_gather(flat, ("dp", "seq"), axis=0, tiled=True)
    lane = 128
    sources = every.shape[0] // flat.shape[0]
    tiles = every.reshape(sources, flat.shape[0] // lane, lane)
    wholes = []
    start = 0
    for piece in pieces:
        size = piece.size
        part = tiles[:, start // lane : (start + size) // lane, :]
        wholes.append(part.reshape(sources * piece.shape[0], piece.shape[1]))
        start += size
    return wholes


def weight_dot(rows, weight):
    return jnp.dot(rows, weight, preferred_element_type=jnp.float32)


def shards(
    voxels,
    patch_weight,
    patch_bias,
    enc_position,
    visible,
    enc_project,
    enc_merge,
    dec_lift,
    mask_token,
    dec_position,
    dec_project,
    dec_merge,
    dec_predict,
):
    seq_count = lax.axis_size("seq")
    seq_place = lax.axis_index("seq")
    enc_parts = max(seq_count // ENC_HEADS, 1)
    dec_parts = max(seq_count // DEC_HEADS, 1)
    enc_part = seq_place % enc_parts
    dec_part = seq_place % dec_parts
    project_rows, project_width = enc_project.shape
    tile_rows = 2 * project_rows
    partner = lax.ppermute(
        enc_project, "seq", perm=[(place, place ^ 1) for place in range(seq_count)]
    )
    half = seq_place % 2
    tile_block = jnp.where(
        half == 0,
        jnp.concatenate([enc_project, partner], axis=0),
        jnp.concatenate([partner, enc_project], axis=0),
    )
    own_width = project_width // 2
    own_block = lax.dynamic_slice_in_dim(tile_block, half * own_width, own_width, axis=1)
    own_block = own_block.reshape(tile_rows, own_width // 128, 128).transpose(1, 0, 2).reshape(-1, 128)
    (tiled_project, full_merge, full_lift, *dec_weights) = gather_weights(
        (own_block, enc_merge, dec_lift, dec_project, dec_merge, dec_predict)
    )
    full_project = (
        tiled_project.reshape(-1, 2, own_width // 128, tile_rows, 128)
        .transpose(0, 3, 1, 2, 4)
        .reshape(-1, project_width)
    )
    tok_local = voxels.shape[1]
    slab_max = tok_local // 2
    slot_ids = jnp.arange(slab_max, dtype=jnp.int32)
    cube_index = 0
    cube_flags = visible[cube_index]
    embedded = (
        jnp.dot(voxels[cube_index], patch_weight, preferred_element_type=jnp.float32)
        + patch_bias
        + enc_position.astype(jnp.float32)
    ).astype(jnp.bfloat16)
    ranking = jnp.cumsum(cube_flags) - 1
    slot_index = jnp.where(cube_flags == 1, ranking, slab_max)
    chooser = (slot_index[None, :] == slot_ids[:, None]).astype(jnp.bfloat16)
    kept_rows = jnp.dot(chooser, embedded, preferred_element_type=jnp.float32).astype(jnp.bfloat16)
    present = slot_ids < jnp.sum(cube_flags)
    packed = weight_dot(
        layer_norm(kept_rows.astype(jnp.float32)).astype(jnp.bfloat16), full_project
    ).astype(jnp.bfloat16)
    key_marks = jnp.broadcast_to(present.astype(jnp.bfloat16)[None, :], (seq_count, slab_max))
    outgoing = spread_heads(packed, ENC_HEADS, seq_count)
    incoming = lax.all_to_all(outgoing, "seq", split_axis=0, concat_axis=0, tiled=True)
    incoming, full_merge, full_lift, dec_weights[0] = lax.optimization_barrier(
        (incoming, full_merge, full_lift, dec_weights[0])
    )
    in_marks = lax.all_to_all(key_marks, "seq", split_axis=0, concat_axis=0, tiled=True)
    key_ok = in_marks.reshape(-1) > 0.5
    mixed_part = attend_heads(incoming, key_ok, ENC_HEADS, enc_part, enc_parts)
    returning = place_rows(mixed_part, incoming.shape[0] * incoming.shape[2], enc_part, seq_count)
    returned = lax.all_to_all(returning, "seq", split_axis=0, concat_axis=0, tiled=True)
    mixed_rows = collect_heads(returned, ENC_HEADS, enc_parts)
    encoded = kept_rows.astype(jnp.float32) + weight_dot(mixed_rows, full_merge)
    lifted_list = [
        weight_dot(layer_norm(encoded).astype(jnp.bfloat16), full_lift)
    ]
    rank_list = [ranking]
    cube_index = 0
    cube_flags = visible[cube_index]
    taken_rows = jnp.take(
        lifted_list[cube_index], jnp.clip(rank_list[cube_index], 0, slab_max - 1), axis=0
    )
    dec_in = (
        jnp.where(cube_flags[:, None] == 1, taken_rows, mask_token[None, :])
        + dec_position.astype(jnp.float32)
    ).astype(jnp.bfloat16)
    dec_packed = weight_dot(
        layer_norm(dec_in.astype(jnp.float32)).astype(jnp.bfloat16), dec_weights[0]
    ).astype(jnp.bfloat16)
    outgoing = spread_heads(dec_packed, DEC_HEADS, seq_count)
    incoming = lax.all_to_all(outgoing, "seq", split_axis=0, concat_axis=0, tiled=True)
    incoming, dec_weights[1], dec_weights[2] = lax.optimization_barrier(
        (incoming, dec_weights[1], dec_weights[2])
    )
    mixed_part = attend_heads(incoming, None, DEC_HEADS, dec_part, dec_parts)
    returning = place_rows(mixed_part, incoming.shape[0] * incoming.shape[2], dec_part, seq_count)
    returned = lax.all_to_all(returning, "seq", split_axis=0, concat_axis=0, tiled=True)
    mixed_rows = collect_heads(returned, DEC_HEADS, dec_parts)
    decoded = (
        dec_in.astype(jnp.float32)
        + weight_dot(mixed_rows, dec_weights[1])
    ).astype(jnp.bfloat16)
    predicted = weight_dot(layer_norm(decoded.astype(jnp.float32)).astype(jnp.bfloat16), dec_weights[2])
    target = layer_norm(voxels[cube_index].astype(jnp.float32))
    squared = jnp.mean((predicted - target) * (predicted - target), axis=-1)
    loss_list = [jnp.where(cube_flags == 1, jnp.zeros_like(squared), squared)]
    decoded_list = [decoded]
    return (jnp.stack(decoded_list), jnp.stack(loss_list))


def solution(mesh):
    return jax.shard_map(
        shards,
        mesh=mesh,
        in_specs=(
            P("dp", "seq", None),
            P(),
            P(),
            P("seq", None),
            P("dp", "seq"),
            P(("dp", "seq"), None),
            P(("dp", "seq"), None),
            P(("dp", "seq"), None),
            P(),
            P("seq", None),
            P(("dp", "seq"), None),
            P(("dp", "seq"), None),
            P(("dp", "seq"), None),
        ),
        out_specs=(P("dp", "seq", None), P("dp", "seq")),
        check_vma=False,
    )
```

```python
import math

import jax
import jax.numpy as jnp
from jax import lax
from jax.sharding import PartitionSpec as P

ENC_HEADS = 16
DEC_HEADS = 16


def layer_norm(values):
    centre = values - jnp.mean(values, axis=-1, keepdims=True)
    spread = jnp.mean(centre * centre, axis=-1, keepdims=True)
    return centre * lax.rsqrt(spread + 1e-06)


def attend_rows(queries, key_rows, value_rows, key_ok):
    query_rows, local_heads, head_size = queries.shape
    block_rows = math.gcd(query_rows, 512)
    score_scale = 1.0 / math.sqrt(head_size)
    query_blocks = queries[:, 0].reshape(query_rows // block_rows, block_rows, head_size)
    keys_one = key_rows[:, 0]
    values_one = value_rows[:, 0]

    def one_block(query_block):
        scores = (
            jnp.einsum("qd,kd->qk", query_block, keys_one, preferred_element_type=jnp.float32)
            * score_scale
        )
        if key_ok is not None:
            scores = jnp.where(key_ok[None, :], scores, -1e30)
        top_score = jnp.max(scores, axis=-1, keepdims=True)
        exponent = jnp.exp(scores - top_score)
        weights = (exponent / jnp.sum(exponent, axis=-1, keepdims=True)).astype(jnp.bfloat16)
        return jnp.einsum(
            "qk,kd->qd", weights, values_one, preferred_element_type=jnp.float32
        ).astype(jnp.bfloat16)

    head_outputs = [lax.map(one_block, query_blocks).reshape(query_rows, head_size)]
    return jnp.stack(head_outputs, axis=1)


def spread_heads(packed, heads, seq_count):
    row_count = packed.shape[0]
    head_size = packed.shape[1] // (3 * heads)
    query_parts = max(seq_count // heads, 1)
    local_heads = max(heads // seq_count, 1)
    layout = packed.reshape(row_count, 3, heads, head_size)
    layout = jnp.repeat(layout, query_parts, axis=2)
    layout = layout.reshape(row_count, 3, seq_count, local_heads, head_size).transpose(
        2, 1, 0, 3, 4
    )
    return layout.reshape(seq_count, 3, row_count, local_heads * head_size)


def attend_heads(incoming, key_ok, heads, query_part, query_parts):
    sources, _, row_count, piece_width = incoming.shape
    local_heads = max(heads // sources, 1)
    head_size = piece_width // local_heads
    all_rows = sources * row_count
    thirds = [
        incoming[:, third].reshape(all_rows, local_heads, head_size) for third in range(3)
    ]
    query_rows = all_rows // query_parts
    queries = lax.dynamic_slice_in_dim(thirds[0], query_part * query_rows, query_rows, 0)
    return attend_rows(queries, thirds[1], thirds[2], key_ok)


def place_rows(mixed_part, all_rows, query_part, sources):
    query_rows = mixed_part.shape[0]
    flat_part = mixed_part.reshape(query_rows, -1)
    buffer = jnp.zeros((all_rows, flat_part.shape[1]), jnp.bfloat16)
    buffer = lax.dynamic_update_slice(buffer, flat_part, (query_part * query_rows, 0))
    return buffer.reshape(sources, all_rows // sources, flat_part.shape[1])


def collect_heads(returned, heads, query_parts):
    sources, row_count, piece_width = returned.shape
    local_heads = max(heads // sources, 1)
    head_size = piece_width // local_heads
    arranged = returned.reshape(sources, row_count, local_heads, head_size).transpose(1, 0, 2, 3)
    arranged = arranged.reshape(row_count, heads, query_parts, head_size)
    summed = jnp.sum(arranged.astype(jnp.float32), axis=2).astype(jnp.bfloat16)
    return summed.reshape(row_count, heads * head_size)


def send_blocks(packed, heads, seq_count):
    row_count = packed.shape[0]
    head_size = packed.shape[1] // (3 * heads)
    query_parts = seq_count // heads
    part_rows = row_count // query_parts
    layout = packed.reshape(row_count, 3, heads, head_size)
    queries = layout[:, 0].reshape(query_parts, part_rows, heads, head_size).transpose(2, 0, 1, 3)
    queries = queries.reshape(seq_count, 1, part_rows, head_size)
    pairs = layout[:, 1:].transpose(2, 1, 0, 3).reshape(heads, 2 * query_parts, part_rows, head_size)
    pairs = jnp.broadcast_to(pairs[:, None], (heads, query_parts) + pairs.shape[1:])
    pairs = pairs.reshape(seq_count, 2 * query_parts, part_rows, head_size)
    return jnp.concatenate([queries, pairs], axis=1)


def attend_blocks(incoming, key_ok):
    sources, blocks, part_rows, head_size = incoming.shape
    query_parts = (blocks - 1) // 2
    queries = incoming[:, 0].reshape(sources * part_rows, 1, head_size)
    keys = incoming[:, 1 : 1 + query_parts].reshape(-1, 1, head_size)
    values = incoming[:, 1 + query_parts :].reshape(-1, 1, head_size)
    mixed = attend_rows(queries, keys, values, key_ok)
    return mixed.reshape(sources, part_rows, head_size)


def take_blocks(returned, heads):
    seq_count, part_rows, head_size = returned.shape
    query_parts = seq_count // heads
    arranged = returned.reshape(heads, query_parts, part_rows, head_size).transpose(1, 2, 0, 3)
    return arranged.reshape(query_parts * part_rows, heads * head_size)


def gather_weights(pieces):
    flat = jnp.concatenate([piece.reshape(-1) for piece in pieces])
    every = lax.all_gather(flat, ("dp", "seq"), axis=0, tiled=True)
    lane = 128
    sources = every.shape[0] // flat.shape[0]
    tiles = every.reshape(sources, flat.shape[0] // lane, lane)
    wholes = []
    start = 0
    for piece in pieces:
        size = piece.size
        part = tiles[:, start // lane : (start + size) // lane, :]
        wholes.append(part.reshape(sources * piece.shape[0], piece.shape[1]))
        start += size
    return wholes


def weight_dot(rows, weight):
    return jnp.dot(rows, weight, preferred_element_type=jnp.float32)


def shards(
    voxels,
    patch_weight,
    patch_bias,
    enc_position,
    visible,
    enc_project,
    enc_merge,
    dec_lift,
    mask_token,
    dec_position,
    dec_project,
    dec_merge,
    dec_predict,
):
    seq_count = lax.axis_size("seq")
    seq_place = lax.axis_index("seq")
    enc_parts = max(seq_count // ENC_HEADS, 1)
    dec_parts = max(seq_count // DEC_HEADS, 1)
    enc_part = seq_place % enc_parts
    dec_part = seq_place % dec_parts
    project_rows, project_width = enc_project.shape
    tile_rows = 2 * project_rows
    partner = lax.ppermute(
        enc_project, "seq", perm=[(place, place ^ 1) for place in range(seq_count)]
    )
    half = seq_place % 2
    tile_block = jnp.where(
        half == 0,
        jnp.concatenate([enc_project, partner], axis=0),
        jnp.concatenate([partner, enc_project], axis=0),
    )
    own_width = project_width // 2
    own_block = lax.dynamic_slice_in_dim(tile_block, half * own_width, own_width, axis=1)
    own_block = own_block.reshape(tile_rows, own_width // 128, 128).transpose(1, 0, 2).reshape(-1, 128)
    (tiled_project, full_merge, full_lift, *dec_weights) = gather_weights(
        (own_block, enc_merge, dec_lift, dec_project, dec_merge, dec_predict)
    )
    full_project = (
        tiled_project.reshape(-1, 2, own_width // 128, tile_rows, 128)
        .transpose(0, 3, 1, 2, 4)
        .reshape(-1, project_width)
    )
    tok_local = voxels.shape[1]
    slab_max = tok_local // 2
    slot_ids = jnp.arange(slab_max, dtype=jnp.int32)
    cube_index = 0
    cube_flags = visible[cube_index]
    embedded = (
        jnp.dot(voxels[cube_index], patch_weight, preferred_element_type=jnp.float32)
        + patch_bias
        + enc_position.astype(jnp.float32)
    ).astype(jnp.bfloat16)
    ranking = jnp.cumsum(cube_flags) - 1
    slot_index = jnp.where(cube_flags == 1, ranking, slab_max)
    chooser = (slot_index[None, :] == slot_ids[:, None]).astype(jnp.bfloat16)
    kept_rows = jnp.dot(chooser, embedded, preferred_element_type=jnp.float32).astype(jnp.bfloat16)
    present = slot_ids < jnp.sum(cube_flags)
    packed = weight_dot(
        layer_norm(kept_rows.astype(jnp.float32)).astype(jnp.bfloat16), full_project
    ).astype(jnp.bfloat16)
    key_marks = jnp.broadcast_to(present.astype(jnp.bfloat16)[None, :], (seq_count, slab_max))
    outgoing = send_blocks(packed, ENC_HEADS, seq_count)
    incoming = lax.all_to_all(outgoing, "seq", split_axis=0, concat_axis=0, tiled=True)
    incoming, full_merge, full_lift, dec_weights[0] = lax.optimization_barrier(
        (incoming, full_merge, full_lift, dec_weights[0])
    )
    in_marks = lax.all_to_all(key_marks, "seq", split_axis=0, concat_axis=0, tiled=True)
    key_ok = in_marks.reshape(-1) > 0.5
    returning = attend_blocks(incoming, key_ok)
    returned = lax.all_to_all(returning, "seq", split_axis=0, concat_axis=0, tiled=True)
    mixed_rows = take_blocks(returned, ENC_HEADS)
    encoded = kept_rows.astype(jnp.float32) + weight_dot(mixed_rows, full_merge)
    lifted_list = [
        weight_dot(layer_norm(encoded).astype(jnp.bfloat16), full_lift)
    ]
    rank_list = [ranking]
    cube_index = 0
    cube_flags = visible[cube_index]
    taken_rows = jnp.take(
        lifted_list[cube_index], jnp.clip(rank_list[cube_index], 0, slab_max - 1), axis=0
    )
    dec_in = (
        jnp.where(cube_flags[:, None] == 1, taken_rows, mask_token[None, :])
        + dec_position.astype(jnp.float32)
    ).astype(jnp.bfloat16)
    dec_packed = weight_dot(
        layer_norm(dec_in.astype(jnp.float32)).astype(jnp.bfloat16), dec_weights[0]
    ).astype(jnp.bfloat16)
    outgoing = send_blocks(dec_packed, DEC_HEADS, seq_count)
    incoming = lax.all_to_all(outgoing, "seq", split_axis=0, concat_axis=0, tiled=True)
    incoming, dec_weights[1], dec_weights[2] = lax.optimization_barrier(
        (incoming, dec_weights[1], dec_weights[2])
    )
    returning = attend_blocks(incoming, None)
    returned = lax.all_to_all(returning, "seq", split_axis=0, concat_axis=0, tiled=True)
    mixed_rows = take_blocks(returned, DEC_HEADS)
    decoded = (
        dec_in.astype(jnp.float32)
        + weight_dot(mixed_rows, dec_weights[1])
    ).astype(jnp.bfloat16)
    predicted = weight_dot(layer_norm(decoded.astype(jnp.float32)).astype(jnp.bfloat16), dec_weights[2])
    target = layer_norm(voxels[cube_index].astype(jnp.float32))
    squared = jnp.mean((predicted - target) * (predicted - target), axis=-1)
    loss_list = [jnp.where(cube_flags == 1, jnp.zeros_like(squared), squared)]
    decoded_list = [decoded]
    return (jnp.stack(decoded_list), jnp.stack(loss_list))


def solution(mesh):
    return jax.shard_map(
        shards,
        mesh=mesh,
        in_specs=(
            P("dp", "seq", None),
            P(),
            P(),
            P("seq", None),
            P("dp", "seq"),
            P(("dp", "seq"), None),
            P(("dp", "seq"), None),
            P(("dp", "seq"), None),
            P(),
            P("seq", None),
            P(("dp", "seq"), None),
            P(("dp", "seq"), None),
            P(("dp", "seq"), None),
        ),
        out_specs=(P("dp", "seq", None), P("dp", "seq")),
        check_vma=False,
    )
```

```python
import math

import jax
import jax.numpy as jnp
from jax import lax
from jax.sharding import PartitionSpec as P

ENC_HEADS = 16
DEC_HEADS = 16


def layer_norm(values):
    centre = values - jnp.mean(values, axis=-1, keepdims=True)
    spread = jnp.mean(centre * centre, axis=-1, keepdims=True)
    return centre * lax.rsqrt(spread + 1e-06)


def attend_rows(queries, key_rows, value_rows, key_ok):
    query_rows, local_heads, head_size = queries.shape
    block_rows = math.gcd(query_rows, 512)
    score_scale = 1.0 / math.sqrt(head_size)
    query_blocks = queries[:, 0].reshape(query_rows // block_rows, block_rows, head_size)
    keys_one = key_rows[:, 0]
    values_one = value_rows[:, 0]

    def one_block(query_block):
        scores = (
            jnp.einsum("qd,kd->qk", query_block, keys_one, preferred_element_type=jnp.float32)
            * score_scale
        )
        if key_ok is not None:
            scores = jnp.where(key_ok[None, :], scores, -1e30)
        top_score = jnp.max(scores, axis=-1, keepdims=True)
        exponent = jnp.exp(scores - top_score)
        weights = (exponent / jnp.sum(exponent, axis=-1, keepdims=True)).astype(jnp.bfloat16)
        return jnp.einsum(
            "qk,kd->qd", weights, values_one, preferred_element_type=jnp.float32
        ).astype(jnp.bfloat16)

    head_outputs = [lax.map(one_block, query_blocks).reshape(query_rows, head_size)]
    return jnp.stack(head_outputs, axis=1)


def spread_heads(packed, heads, seq_count):
    row_count = packed.shape[0]
    head_size = packed.shape[1] // (3 * heads)
    query_parts = max(seq_count // heads, 1)
    local_heads = max(heads // seq_count, 1)
    layout = packed.reshape(row_count, 3, heads, head_size)
    layout = jnp.repeat(layout, query_parts, axis=2)
    layout = layout.reshape(row_count, 3, seq_count, local_heads, head_size).transpose(
        2, 1, 0, 3, 4
    )
    return layout.reshape(seq_count, 3, row_count, local_heads * head_size)


def attend_heads(incoming, key_ok, heads, query_part, query_parts):
    sources, _, row_count, piece_width = incoming.shape
    local_heads = max(heads // sources, 1)
    head_size = piece_width // local_heads
    all_rows = sources * row_count
    thirds = [
        incoming[:, third].reshape(all_rows, local_heads, head_size) for third in range(3)
    ]
    query_rows = all_rows // query_parts
    queries = lax.dynamic_slice_in_dim(thirds[0], query_part * query_rows, query_rows, 0)
    return attend_rows(queries, thirds[1], thirds[2], key_ok)


def place_rows(mixed_part, all_rows, query_part, sources):
    query_rows = mixed_part.shape[0]
    flat_part = mixed_part.reshape(query_rows, -1)
    buffer = jnp.zeros((all_rows, flat_part.shape[1]), jnp.bfloat16)
    buffer = lax.dynamic_update_slice(buffer, flat_part, (query_part * query_rows, 0))
    return buffer.reshape(sources, all_rows // sources, flat_part.shape[1])


def collect_heads(returned, heads, query_parts):
    sources, row_count, piece_width = returned.shape
    local_heads = max(heads // sources, 1)
    head_size = piece_width // local_heads
    arranged = returned.reshape(sources, row_count, local_heads, head_size).transpose(1, 0, 2, 3)
    arranged = arranged.reshape(row_count, heads, query_parts, head_size)
    summed = jnp.sum(arranged.astype(jnp.float32), axis=2).astype(jnp.bfloat16)
    return summed.reshape(row_count, heads * head_size)


def send_blocks(packed, heads, seq_count):
    row_count = packed.shape[0]
    head_size = packed.shape[1] // (3 * heads)
    query_parts = seq_count // heads
    part_rows = row_count // query_parts
    layout = packed.reshape(row_count, 3, heads, head_size)
    queries = layout[:, 0].reshape(query_parts, part_rows, heads, head_size).transpose(2, 0, 1, 3)
    queries = queries.reshape(seq_count, 1, part_rows, head_size)
    pairs = layout[:, 1:].transpose(2, 1, 0, 3).reshape(heads, 2 * query_parts, part_rows, head_size)
    pairs = jnp.broadcast_to(pairs[:, None], (heads, query_parts) + pairs.shape[1:])
    pairs = pairs.reshape(seq_count, 2 * query_parts, part_rows, head_size)
    return jnp.concatenate([queries, pairs], axis=1)


def attend_blocks(incoming, key_ok):
    sources, blocks, part_rows, head_size = incoming.shape
    query_parts = (blocks - 1) // 2
    queries = incoming[:, 0].reshape(sources * part_rows, 1, head_size)
    keys = incoming[:, 1 : 1 + query_parts].reshape(-1, 1, head_size)
    values = incoming[:, 1 + query_parts :].reshape(-1, 1, head_size)
    mixed = attend_rows(queries, keys, values, key_ok)
    return mixed.reshape(sources, part_rows, head_size)


def take_blocks(returned, heads):
    seq_count, part_rows, head_size = returned.shape
    query_parts = seq_count // heads
    arranged = returned.reshape(heads, query_parts, part_rows, head_size).transpose(1, 2, 0, 3)
    return arranged.reshape(query_parts * part_rows, heads * head_size)


def gather_weights(pieces):
    flat = jnp.concatenate([piece.reshape(-1) for piece in pieces])
    every = lax.all_gather(flat, ("dp", "seq"), axis=0, tiled=True)
    lane = 128
    sources = every.shape[0] // flat.shape[0]
    tiles = every.reshape(sources, flat.shape[0] // lane, lane)
    wholes = []
    start = 0
    for piece in pieces:
        size = piece.size
        part = tiles[:, start // lane : (start + size) // lane, :]
        wholes.append(part.reshape(sources * piece.shape[0], piece.shape[1]))
        start += size
    return wholes


def weight_dot(rows, weight):
    return jnp.dot(rows, weight, preferred_element_type=jnp.float32)


def shards(
    voxels,
    patch_weight,
    patch_bias,
    enc_position,
    visible,
    enc_project,
    enc_merge,
    dec_lift,
    mask_token,
    dec_position,
    dec_project,
    dec_merge,
    dec_predict,
):
    seq_count = lax.axis_size("seq")
    seq_place = lax.axis_index("seq")
    enc_parts = max(seq_count // ENC_HEADS, 1)
    dec_parts = max(seq_count // DEC_HEADS, 1)
    enc_part = seq_place % enc_parts
    dec_part = seq_place % dec_parts
    project_rows, project_width = enc_project.shape
    tile_rows = 2 * project_rows
    partner = lax.ppermute(
        enc_project, "seq", perm=[(place, place ^ 1) for place in range(seq_count)]
    )
    half = seq_place % 2
    tile_block = jnp.where(
        half == 0,
        jnp.concatenate([enc_project, partner], axis=0),
        jnp.concatenate([partner, enc_project], axis=0),
    )
    own_width = project_width // 2
    own_block = lax.dynamic_slice_in_dim(tile_block, half * own_width, own_width, axis=1)
    own_block = own_block.reshape(tile_rows, own_width // 128, 128).transpose(1, 0, 2).reshape(-1, 128)
    (tiled_project, full_merge, full_lift, *dec_weights) = gather_weights(
        (own_block, enc_merge, dec_lift, dec_project, dec_merge, dec_predict)
    )
    full_project = (
        tiled_project.reshape(-1, 2, own_width // 128, tile_rows, 128)
        .transpose(0, 3, 1, 2, 4)
        .reshape(-1, project_width)
    )
    tok_local = voxels.shape[1]
    slab_max = tok_local // 2
    slot_ids = jnp.arange(slab_max, dtype=jnp.int32)
    cube_index = 0
    cube_flags = visible[cube_index]
    embedded = (
        jnp.dot(voxels[cube_index], patch_weight, preferred_element_type=jnp.float32)
        + patch_bias
        + enc_position.astype(jnp.float32)
    ).astype(jnp.bfloat16)
    ranking = jnp.cumsum(cube_flags) - 1
    slot_index = jnp.where(cube_flags == 1, ranking, slab_max)
    chooser = (slot_index[None, :] == slot_ids[:, None]).astype(jnp.bfloat16)
    kept_rows = jnp.dot(chooser, embedded, preferred_element_type=jnp.float32).astype(jnp.bfloat16)
    present = slot_ids < jnp.sum(cube_flags)
    packed = weight_dot(
        layer_norm(kept_rows.astype(jnp.float32)).astype(jnp.bfloat16), full_project
    ).astype(jnp.bfloat16)
    key_marks = jnp.broadcast_to(present.astype(jnp.bfloat16)[None, :], (seq_count, slab_max))
    outgoing = send_blocks(packed, ENC_HEADS, seq_count)
    incoming = lax.all_to_all(outgoing, "seq", split_axis=0, concat_axis=0, tiled=True)
    incoming, full_merge, full_lift = lax.optimization_barrier((incoming, full_merge, full_lift))
    in_marks = lax.all_to_all(key_marks, "seq", split_axis=0, concat_axis=0, tiled=True)
    key_ok = in_marks.reshape(-1) > 0.5
    returning = attend_blocks(incoming, key_ok)
    returned = lax.all_to_all(returning, "seq", split_axis=0, concat_axis=0, tiled=True)
    returned, dec_weights[0] = lax.optimization_barrier((returned, dec_weights[0]))
    mixed_rows = take_blocks(returned, ENC_HEADS)
    encoded = kept_rows.astype(jnp.float32) + weight_dot(mixed_rows, full_merge)
    lifted_list = [
        weight_dot(layer_norm(encoded).astype(jnp.bfloat16), full_lift)
    ]
    rank_list = [ranking]
    cube_index = 0
    cube_flags = visible[cube_index]
    taken_rows = jnp.take(
        lifted_list[cube_index], jnp.clip(rank_list[cube_index], 0, slab_max - 1), axis=0
    )
    dec_in = (
        jnp.where(cube_flags[:, None] == 1, taken_rows, mask_token[None, :])
        + dec_position.astype(jnp.float32)
    ).astype(jnp.bfloat16)
    dec_packed = weight_dot(
        layer_norm(dec_in.astype(jnp.float32)).astype(jnp.bfloat16), dec_weights[0]
    ).astype(jnp.bfloat16)
    outgoing = send_blocks(dec_packed, DEC_HEADS, seq_count)
    incoming = lax.all_to_all(outgoing, "seq", split_axis=0, concat_axis=0, tiled=True)
    incoming, dec_weights[1], dec_weights[2] = lax.optimization_barrier(
        (incoming, dec_weights[1], dec_weights[2])
    )
    returning = attend_blocks(incoming, None)
    returned = lax.all_to_all(returning, "seq", split_axis=0, concat_axis=0, tiled=True)
    mixed_rows = take_blocks(returned, DEC_HEADS)
    decoded = (
        dec_in.astype(jnp.float32)
        + weight_dot(mixed_rows, dec_weights[1])
    ).astype(jnp.bfloat16)
    predicted = weight_dot(layer_norm(decoded.astype(jnp.float32)).astype(jnp.bfloat16), dec_weights[2])
    target = layer_norm(voxels[cube_index].astype(jnp.float32))
    squared = jnp.mean((predicted - target) * (predicted - target), axis=-1)
    loss_list = [jnp.where(cube_flags == 1, jnp.zeros_like(squared), squared)]
    decoded_list = [decoded]
    return (jnp.stack(decoded_list), jnp.stack(loss_list))


def solution(mesh):
    return jax.shard_map(
        shards,
        mesh=mesh,
        in_specs=(
            P("dp", "seq", None),
            P(),
            P(),
            P("seq", None),
            P("dp", "seq"),
            P(("dp", "seq"), None),
            P(("dp", "seq"), None),
            P(("dp", "seq"), None),
            P(),
            P("seq", None),
            P(("dp", "seq"), None),
            P(("dp", "seq"), None),
            P(("dp", "seq"), None),
        ),
        out_specs=(P("dp", "seq", None), P("dp", "seq")),
        check_vma=False,
    )
```
